32 devices in a mesh: row: 8 (over y, x, core), col: 4 (over z).
Axes of the slice: x: 2, y: 2, z: 4, core: 2. Of those that a mesh axis runs over, the one named last changes fastest.
Arguments:
- queries: bfloat16 [512, 2, 2048], P('row', None, 'col'), may hold values from -15 to 15
- new_keys: bfloat16 [512, 2, 2048], P('row', None, 'col'), may hold values from -6 to 6
- new_values: bfloat16 [512, 2, 2048], P('row', None, 'col'), may hold values from -6 to 6
- cache_keys: bfloat16 [1024, 2, 2048], P('row', None, 'col'), may hold values from -6 to 6
- cache_values: bfloat16 [1024, 2, 2048], P('row', None, 'col'), may hold values from -6 to 6
- cached_len: int32 [2], replicated, may hold values from 256 to 1024, as said below
- residual: bfloat16 [512, 2, 2048], P('row'), may hold values from -4 to 4
- out_weight: bfloat16 [2048, 2048], P('col'), may hold values from -0.125 to 0.125
- norm_gain: float32 [2048], replicated, may hold values from 0.5 to 1.5
- expert_ids: int32 [512, 2, 6], P('row'), may hold values from 0 to 63, all different within a row; in each aligned block of 128 rows (0 to 127, 128 to 255, ..., all dimensions but the last counted through in order) at most 24 rows name the same one
- gate_values: float32 [512, 2, 6], P('row'), may hold values from 0.1 to 0.6
- w_gate: bfloat16 [256, 2048, 352], P(('row', 'col')), may hold values from -0.125 to 0.125
- w_up: bfloat16 [256, 2048, 352], P(('row', 'col')), may hold values from -0.125 to 0.125
- w_down: bfloat16 [256, 352, 2048], P(('row', 'col')), may hold values from -0.15625 to 0.15625
- shared_gate: bfloat16 [2048, 2816], P(None, 'col'), may hold values from -0.125 to 0.125
- shared_up: bfloat16 [2048, 2816], P(None, 'col'), may hold values from -0.125 to 0.125
- shared_down: bfloat16 [2816, 2048], P('col'), may hold values from -0.109375 to 0.109375
Outputs:
- mixed: bfloat16 [512, 2, 2048], P('row', None, 'col')
- ffn_out: bfloat16 [512, 2, 2048], P('row', None, 'col')
The draws below stay inside these ranges and needn't reach their ends.
Inputs may be any that keep to these rules, and one draw needn't show every extreme that they name: `cached_len`: some request has exactly 1024 cached positions. `expert_ids`: each token names 6 different experts. Among the 128 tokens of one index of row (positions taken in order, requests inside), no expert is named more than 24 times, and in some such blocks one expert is named exactly 24 times.
All inputs are finite; a program needn't handle non-finite values.
Results may differ from the reference program's by a relative error of at most 0.023.
Values may be sent and summed in bfloat16 or wider, within the bound.
No kernel may reach another device: no remote copies, remote signals or barrier semaphores. Data moves between devices by JAX's collectives and lax.ppermute only.
A program may use at most 192 MiB of HBM per device.

```python
import math
import jax
import jax.numpy as jnp
import numpy as np
from jax import lax

D = 2048
H = 16
HD = 128
E = 64
FE = 1408
SHARED = 2816
TOPK = 6
GROUPS = 4
R = 2
NEW = 512
CACHE = 1024
TOK_DEV = 128
CAP = 24
N_ROW = 8


def draw_queries(key, part):
    full_shape = (NEW, R, H * HD)
    values = jnp.clip(2.5 * jax.random.normal(jax.random.fold_in(key, 11), full_shape, jnp.float32), -15.0, 15.0)
    return values.astype(jnp.bfloat16)


def draw_cache_keys(key, part):
    full_shape = (CACHE, R, H * HD)
    values = jnp.clip(jax.random.normal(jax.random.fold_in(key, 12), full_shape, jnp.float32), -6.0, 6.0)
    return values.astype(jnp.bfloat16)


def draw_cached_len(key, part):
    lengths = jax.random.randint(jax.random.fold_in(key, 13), (R,), CACHE // 4, CACHE + 1, dtype=jnp.int32)
    longest = jax.random.randint(jax.random.fold_in(key, 14), (), 0, R, dtype=jnp.int32)
    return jnp.where(jnp.arange(R, dtype=jnp.int32) == longest, CACHE, lengths).astype(jnp.int32)


def block_levels(stream_key, shape, split, least, high):
    level, own = 1.0, jax.random.fold_in(stream_key, 6)
    for dim, shards_of in split:
        draws = jnp.exp(jax.random.uniform(jax.random.fold_in(own, dim), (shards_of,), jnp.float32, least / len(split), high / len(split)))
        level = level * jnp.repeat(draws, shape[dim] // shards_of).reshape([-1 if axis == dim else 1 for axis in range(len(shape))])
    return level


def assign_block(own_key, own, number, rows, amount, top, reach, slope):
    order = jax.random.permutation(own_key, amount)
    heavy_load, ordinary = portions_of(amount, rows * top, reach, slope, True), portions_of(amount, rows * top, reach, slope, False)
    places = jnp.arange(amount)

    def named(sizes, turn):
        used = int((sizes > 0).sum())
        fixed = max(1, used // 4)
        shifted = fixed + (places - fixed + turn * (used - fixed)) % max(1, amount - fixed)
        return jnp.zeros((amount,), jnp.int32).at[order[jnp.where(places < fixed, places, shifted)]].set(jnp.asarray(sizes, jnp.int32))

    sizes = jnp.where(number % 4 == 0, named(heavy_load, number // 4), named(ordinary, number - number // 4 - 1))
    mixed = jax.random.permutation(jax.random.fold_in(own, 3), amount)
    giver, sink = mixed[0:amount // 2 * 2:2], mixed[1:amount // 2 * 2:2]
    room = jnp.minimum(sizes[giver] - 1, reach - sizes[sink]) // 2
    room = jnp.where((giver == order[0]) | (sink == order[0]) | (sizes[sink] == 0), 0, jnp.maximum(room, 0))
    shifted = jax.random.randint(jax.random.fold_in(own, 4), (amount // 2,), 0, 1 << 20) % (room + 1)
    sizes = sizes.at[giver].add(-shifted).at[sink].add(shifted)
    items = jnp.searchsorted(jnp.cumsum(sizes), jnp.arange(rows * top), side="right").astype(jnp.int32)
    grid = items.reshape(top, rows).T
    grid = grid[jax.random.permutation(jax.random.fold_in(own, 1), rows)]
    turn = jax.random.randint(jax.random.fold_in(own, 2), (rows, 1), 0, top)
    return jnp.take_along_axis(grid, (jnp.arange(top)[None, :] + turn) % top, axis=1)


def portions_of(number_of, total, most, slope, full):
    loads = [(1 << 20) // math.isqrt(rank ** slope) + 1 for rank in range(1, number_of + 1)]
    largest = most if full else min(most, max(-(-total // number_of), total * loads[0] // sum(loads)))
    least = 1 if total - largest >= number_of - 1 else 0
    given, surplus = [largest] + [least] * (number_of - 1), total - largest - least * (number_of - 1)
    while surplus > 0:
        movable = [i for i in range(1, number_of) if given[i] < largest] or [i for i in range(1, number_of) if given[i] < most]
        pool, left = sum([loads[i] for i in movable]), surplus
        for i in movable:
            more = min(most - given[i], max(1, left * loads[i] // pool), surplus)
            given[i] = given[i] + more
            surplus = surplus - more
    return np.array(given)


def centred(stream_key, shape, spread, most, shards=(), kind=jnp.bfloat16):
    result = jax.random.normal(stream_key, shape, jnp.float32) * spread
    if len(shards) > 0:
        result = block_levels(stream_key, shape, shards, -0.22, 0.18) * result
    return jnp.clip(result, min=-most, max=most).astype(kind)


def setup_inputs(seed: int = 0) -> dict:
    arg_keys = jax.random.split(jax.random.key(seed), 18)
    queries = draw_queries(jax.random.fold_in(arg_keys[17], 71), 0)
    new_keys = centred(arg_keys[1], (NEW, R, H * HD), 1.0, 6.0, ((0, 8), (2, 4)))
    new_values = centred(arg_keys[2], (NEW, R, H * HD), 1.0, 6.0, ((0, 8), (2, 4)))
    cache_keys = draw_cache_keys(jax.random.fold_in(arg_keys[17], 71), 0)
    cache_values = centred(arg_keys[4], (CACHE, R, H * HD), 1.0, 6.0, ((0, 8), (2, 4)))
    cached_len = draw_cached_len(jax.random.fold_in(arg_keys[17], 71), 0)
    residual = centred(arg_keys[6], (NEW, R, D), 0.3, 4.0, ((0, 8),))
    out_weight = centred(arg_keys[7], (H * HD, D), (H * HD) ** -0.5, 0.125, ((0, 4),))
    norm_gain = jnp.clip(1.0 + 0.1 * jax.random.normal(arg_keys[8], (D,), jnp.float32), 0.5, 1.5)
    expert_ids_keys = jax.random.split(jax.random.fold_in(arg_keys[9], 1), NEW * R // TOK_DEV)
    expert_ids_turns = jax.random.permutation(jax.random.fold_in(arg_keys[9], 3), NEW * R // TOK_DEV)
    expert_ids = jax.vmap(lambda own, number: assign_block(jax.random.fold_in(arg_keys[9], 2), own, number, TOK_DEV, E, TOPK, CAP, 2))(expert_ids_keys, expert_ids_turns).reshape((NEW, R, TOPK))
    gate_values = jnp.clip(jnp.exp(math.log(0.6) - 1.7917595 * jax.random.uniform(arg_keys[10], (NEW, R, TOPK), jnp.float32) ** block_levels(arg_keys[10], (NEW, R, TOPK), ((0, 8),), -0.2, 0.2)), 0.1, 0.6)
    w_gate = centred(arg_keys[11], (E * GROUPS, D, FE // GROUPS), D ** -0.5, 0.125, ((0, 32),))
    w_up = centred(arg_keys[12], (E * GROUPS, D, FE // GROUPS), D ** -0.5, 0.125, ((0, 32),))
    w_down = centred(arg_keys[13], (E * GROUPS, FE // GROUPS, D), FE ** -0.5, 0.15625, ((0, 32),))
    shared_gate = centred(arg_keys[14], (D, SHARED), D ** -0.5, 0.125, ((1, 4),))
    shared_up = centred(arg_keys[15], (D, SHARED), D ** -0.5, 0.125, ((1, 4),))
    shared_down = centred(arg_keys[16], (SHARED, D), SHARED ** -0.5, 0.109375, ((0, 4),))
    return {"queries": queries, "new_keys": new_keys, "new_values": new_values, "cache_keys": cache_keys, "cache_values": cache_values, "cached_len": cached_len, "residual": residual, "out_weight": out_weight, "norm_gain": norm_gain, "expert_ids": expert_ids, "gate_values": gate_values, "w_gate": w_gate, "w_up": w_up, "w_down": w_down, "shared_gate": shared_gate, "shared_up": shared_up, "shared_down": shared_down}


def reference(queries, new_keys, new_values, cache_keys, cache_values, cached_len, residual, out_weight, norm_gain, expert_ids, gate_values, w_gate, w_up, w_down, shared_gate, shared_up, shared_down):
    total_pos = CACHE + NEW
    all_keys = jnp.concatenate([cache_keys, new_keys], axis=0).reshape(total_pos, R, H, HD)
    all_values = jnp.concatenate([cache_values, new_values], axis=0).reshape(total_pos, R, H, HD)
    query_heads = queries.reshape(NEW, R, H, HD)
    key_pos = jnp.arange(total_pos, dtype=jnp.int32)
    query_pos = jnp.arange(NEW, dtype=jnp.int32)
    in_cache = key_pos < CACHE
    cache_ok = in_cache[None, :] & (key_pos[None, :] < cached_len[:, None])
    new_ok = jnp.logical_not(in_cache)[None, :] & ((key_pos - CACHE)[None, :] <= query_pos[:, None])
    allowed = cache_ok[:, None, :] | new_ok[None, :, :]
    score_scale = 1.0 / math.sqrt(HD)

    def one_head(head_index):
        q_head = lax.dynamic_index_in_dim(query_heads, head_index, 2, keepdims=False).astype(jnp.float32)
        k_head = lax.dynamic_index_in_dim(all_keys, head_index, 2, keepdims=False).astype(jnp.float32)
        v_head = lax.dynamic_index_in_dim(all_values, head_index, 2, keepdims=False).astype(jnp.float32)
        scores = jnp.einsum('ird,jrd->rij', q_head, k_head) * score_scale
        masked = jnp.where(allowed, scores, -1e+30)
        row_top = lax.optimization_barrier(jnp.max(masked, axis=-1, keepdims=True))
        weights = jnp.where(allowed, jnp.exp(masked - row_top), 0.0)
        weight_total = lax.optimization_barrier(jnp.sum(weights, axis=-1))
        rounded = lax.optimization_barrier(weights.astype(jnp.bfloat16)).astype(jnp.float32)
        summed = jnp.einsum('rij,jrd->ird', rounded, v_head)
        return (summed / jnp.transpose(weight_total)[:, :, None]).astype(jnp.bfloat16)
    attended = lax.map(one_head, jnp.arange(H, dtype=jnp.int32))
    tokens = NEW * R
    attended = jnp.transpose(attended, (1, 2, 0, 3)).reshape(tokens, H * HD)
    attn_out = jnp.dot(attended, out_weight, preferred_element_type=jnp.float32)
    mixed = (residual.reshape(tokens, D).astype(jnp.float32) + attn_out).astype(jnp.bfloat16)
    mixed_f = mixed.astype(jnp.float32)
    normed = (mixed_f * lax.rsqrt(lax.optimization_barrier(jnp.mean(mixed_f * mixed_f, axis=-1, keepdims=True)) + 1e-06) * norm_gain).astype(jnp.bfloat16)
    chosen = expert_ids.reshape(tokens * TOPK).astype(jnp.int32)
    onehot = (chosen[:, None] == jnp.arange(E, dtype=jnp.int32)[None, :]).astype(jnp.int32)
    running = jnp.cumsum(onehot.reshape(N_ROW, TOK_DEV * TOPK, E), axis=1).reshape(tokens * TOPK, E)
    slot_index = lax.optimization_barrier(jnp.sum(running * onehot, axis=1)) - 1
    owner_block = jnp.arange(tokens * TOPK, dtype=jnp.int32) // (TOK_DEV * TOPK)
    place_index = (owner_block * CAP + slot_index).astype(jnp.int32)
    repeated = jnp.repeat(normed, TOPK, axis=0)
    dispatched = jnp.zeros((E, N_ROW * CAP, D), jnp.bfloat16).at[chosen, place_index].set(repeated)

    def one_expert(expert):
        first = (expert * GROUPS).astype(jnp.int32)
        rows_in = lax.dynamic_index_in_dim(dispatched, expert, 0, keepdims=False).astype(jnp.float32)
        gate_e = lax.dynamic_slice_in_dim(w_gate, first, GROUPS, 0).astype(jnp.float32)
        up_e = lax.dynamic_slice_in_dim(w_up, first, GROUPS, 0).astype(jnp.float32)
        down_e = lax.dynamic_slice_in_dim(w_down, first, GROUPS, 0).astype(jnp.float32)
        gate_proj = jnp.einsum('sd,gdf->sgf', rows_in, gate_e)
        up_proj = jnp.einsum('sd,gdf->sgf', rows_in, up_e)
        hidden_act = lax.optimization_barrier((jax.nn.silu(gate_proj) * up_proj).astype(jnp.bfloat16)).astype(jnp.float32)
        group_parts = jnp.einsum('sgf,gfd->sgd', hidden_act, down_e)
        group_parts = lax.optimization_barrier(group_parts.astype(jnp.bfloat16)).astype(jnp.float32)
        return lax.optimization_barrier(jnp.sum(group_parts, axis=1))
    outputs = lax.map(one_expert, jnp.arange(E, dtype=jnp.int32))
    picked = outputs[chosen, place_index]
    routed = lax.optimization_barrier(jnp.sum(picked.reshape(tokens, TOPK, D) * gate_values.reshape(tokens, TOPK, 1), axis=1))
    shared_g = jnp.dot(normed, shared_gate, preferred_element_type=jnp.float32)
    shared_u = jnp.dot(normed, shared_up, preferred_element_type=jnp.float32)
    shared_act = (jax.nn.silu(shared_g) * shared_u).astype(jnp.bfloat16)
    shared_out = jnp.dot(shared_act, shared_down, preferred_element_type=jnp.float32)
    ffn_out = (routed + shared_out).astype(jnp.bfloat16)
    return (mixed.reshape(NEW, R, D), ffn_out.reshape(NEW, R, D))
```

```python
import math

import jax
import jax.numpy as jnp
from jax import lax
from jax.sharding import PartitionSpec as P

HD = 128
E = 64
TOPK = 6
GROUPS = 4
CAP = 24


def body(
    queries,
    new_keys,
    new_values,
    cache_keys,
    cache_values,
    cached_len,
    residual,
    out_weight,
    norm_gain,
    expert_ids,
    gate_values,
    w_gate,
    w_up,
    w_down,
    shared_gate,
    shared_up,
    shared_down,
):
    rows_here = queries.shape[0]
    requests = queries.shape[1]
    heads_here = queries.shape[2] // HD
    cache_rows = cache_keys.shape[0]
    block_rows = cache_rows + rows_here
    model_width = residual.shape[2]
    row_index = lax.axis_index("row")
    row_count = lax.axis_size("row")
    score_scale = 1.0 / math.sqrt(HD)
    keys_here = jnp.concatenate([cache_keys, new_keys], axis=0)
    values_here = jnp.concatenate([cache_values, new_values], axis=0)
    query_heads = queries.reshape(rows_here, requests, heads_here, HD)
    local_pos = row_index * rows_here + jnp.arange(rows_here, dtype=jnp.int32)
    key_piece = lax.all_gather(keys_here, "row", axis=0, tiled=True)
    key_count = key_piece.shape[0]
    global_row = jnp.arange(key_count, dtype=jnp.int32)
    shard_index = global_row // block_rows
    offset_rows = global_row % block_rows
    in_cache = offset_rows < cache_rows
    cache_pos = shard_index * cache_rows + offset_rows
    new_pos = shard_index * rows_here + offset_rows - cache_rows
    cache_ok = in_cache[None, :] & (cache_pos[None, :] < cached_len[:, None])
    new_ok = jnp.logical_not(in_cache)[None, :] & (new_pos[None, :] <= local_pos[:, None])
    allowed = cache_ok[:, None, None, :] | new_ok[None, None, :, :]
    key_heads = key_piece.reshape(key_count, requests, heads_here, HD)
    value_heads = lax.all_gather(values_here, "row", axis=0, tiled=True).reshape(
        key_count, requests, heads_here, HD
    )
    scores = (
        jnp.einsum("irhd,jrhd->rhij", query_heads, key_heads, preferred_element_type=jnp.float32)
        * score_scale
    )
    masked = jnp.where(allowed, scores, -1e30)
    old_max = jnp.full((requests, heads_here, rows_here), -1e30, jnp.float32)
    new_max = jnp.maximum(old_max, jnp.max(masked, axis=-1))
    weights_now = jnp.where(allowed, jnp.exp(masked - new_max[..., None]), 0.0)
    new_sum = jnp.sum(weights_now, axis=-1)
    product = jnp.einsum(
        "rhij,jrhd->rhid",
        weights_now.astype(jnp.bfloat16),
        value_heads,
        preferred_element_type=jnp.float32,
    )
    attended = (product / new_sum[..., None]).astype(jnp.bfloat16)
    head_weights = out_weight.reshape(heads_here, HD, model_width)
    attn_part = jnp.einsum(
        "rhid,hde->ire", attended, head_weights, preferred_element_type=jnp.float32
    )
    attn_full = lax.psum(attn_part.astype(jnp.bfloat16), "col").astype(jnp.float32)
    mixed_full = (residual.astype(jnp.float32) + attn_full).astype(jnp.bfloat16)
    mixed_f32 = mixed_full.astype(jnp.float32)
    normed = (
        mixed_f32
        * lax.rsqrt(jnp.mean(mixed_f32 * mixed_f32, axis=-1, keepdims=True) + 1e-06)
        * norm_gain
    ).astype(jnp.bfloat16)
    token_count = rows_here * requests
    tokens = normed.reshape(token_count, model_width)
    col_index = lax.axis_index("col")
    col_count = lax.axis_size("col")
    entries_here = w_gate.shape[0]
    experts_dev = max(1, entries_here // GROUPS)
    groups_dev = entries_here // experts_dev
    experts_per_row = col_count * entries_here // GROUPS
    slots = row_count * experts_dev * CAP
    chosen = expert_ids.reshape(token_count * TOPK)
    onehot = (chosen[:, None] == jnp.arange(E, dtype=jnp.int32)[None, :]).astype(jnp.int32)
    slot_index = jnp.sum(jnp.cumsum(onehot, axis=0) * onehot, axis=1) - 1
    dest_row = chosen // experts_per_row
    local_expert = chosen - (dest_row * col_count + col_index) * entries_here // GROUPS
    valid = (local_expert >= 0) & (local_expert < experts_dev)
    place = (dest_row * experts_dev + local_expert) * CAP + slot_index
    place = jnp.where(valid, place, -1).reshape(token_count, TOPK)
    hit = place[:, :, None] == jnp.arange(slots, dtype=jnp.int32)[None, None, :]
    dispatch = jnp.sum(hit.astype(jnp.float32), axis=1).astype(jnp.bfloat16)
    combine = jnp.sum(
        jnp.where(hit, gate_values.reshape(token_count, TOPK, 1), 0.0), axis=1
    )
    outgoing = lax.dot_general(
        dispatch, tokens, (((0,), (0,)), ((), ())), preferred_element_type=jnp.float32
    ).astype(jnp.bfloat16)
    outgoing = outgoing.reshape(row_count, experts_dev, CAP, model_width)
    arrived = lax.all_to_all(outgoing, "row", 0, 0, tiled=True)
    hidden = w_gate.shape[2]
    wg = w_gate.reshape(experts_dev, groups_dev, model_width, hidden)
    wu = w_up.reshape(experts_dev, groups_dev, model_width, hidden)
    wd = w_down.reshape(experts_dev, groups_dev, hidden, model_width)
    gate_proj = jnp.einsum("nlsd,lgdf->lgnsf", arrived, wg, preferred_element_type=jnp.float32)
    up_proj = jnp.einsum("nlsd,lgdf->lgnsf", arrived, wu, preferred_element_type=jnp.float32)
    hidden_act = (jax.nn.silu(gate_proj) * up_proj).astype(jnp.bfloat16)
    expert_out = jnp.einsum(
        "lgnsf,lgfd->nlsd", hidden_act, wd, preferred_element_type=jnp.float32
    ).astype(jnp.bfloat16)
    returned = lax.all_to_all(expert_out, "row", 0, 0, tiled=True).reshape(slots, model_width)
    combine_hi = combine.astype(jnp.bfloat16)
    combine_lo = (combine - combine_hi.astype(jnp.float32)).astype(jnp.bfloat16)
    routed = jnp.dot(combine_hi, returned, preferred_element_type=jnp.float32) + jnp.dot(
        combine_lo, returned, preferred_element_type=jnp.float32
    )
    shared_g = jnp.dot(tokens, shared_gate, preferred_element_type=jnp.float32)
    shared_u = jnp.dot(tokens, shared_up, preferred_element_type=jnp.float32)
    shared_act = (jax.nn.silu(shared_g) * shared_u).astype(jnp.bfloat16)
    shared_part = jnp.dot(shared_act, shared_down, preferred_element_type=jnp.float32)
    ffn_total = lax.psum_scatter(
        (routed + shared_part).astype(jnp.bfloat16), "col", scatter_dimension=1, tiled=True
    )
    col_width = model_width // col_count
    ffn_here = ffn_total.reshape(rows_here, requests, col_width)
    mixed_here = lax.dynamic_slice_in_dim(mixed_full, col_index * col_width, col_width, 2)
    return (mixed_here, ffn_here)


def solution(mesh):
    in_specs = (
        P("row", None, "col"),
        P("row", None, "col"),
        P("row", None, "col"),
        P("row", None, "col"),
        P("row", None, "col"),
        P(),
        P("row", None, None),
        P("col", None),
        P(),
        P("row", None, None),
        P("row", None, None),
        P(("row", "col"), None, None),
        P(("row", "col"), None, None),
        P(("row", "col"), None, None),
        P(None, "col"),
        P(None, "col"),
        P("col", None),
    )
    out_specs = (P("row", None, "col"), P("row", None, "col"))
    return jax.shard_map(body, mesh=mesh, in_specs=in_specs, out_specs=out_specs, check_vma=False)
```

```python
import math

import jax
import jax.numpy as jnp
from jax import lax
from jax.sharding import PartitionSpec as P

HD = 128
E = 64
TOPK = 6
GROUPS = 4
CAP = 24


def body(
    queries,
    new_keys,
    new_values,
    cache_keys,
    cache_values,
    cached_len,
    residual,
    out_weight,
    norm_gain,
    expert_ids,
    gate_values,
    w_gate,
    w_up,
    w_down,
    shared_gate,
    shared_up,
    shared_down,
):
    rows_here = queries.shape[0]
    requests = queries.shape[1]
    heads_here = queries.shape[2] // HD
    cache_rows = cache_keys.shape[0]
    block_rows = cache_rows + rows_here
    model_width = residual.shape[2]
    row_index = lax.axis_index("row")
    row_count = lax.axis_size("row")
    score_scale = 1.0 / math.sqrt(HD)
    keys_here = jnp.concatenate([cache_keys, new_keys], axis=0).reshape(
        block_rows, requests, heads_here, HD
    )
    values_here = jnp.concatenate([cache_values, new_values], axis=0).reshape(
        block_rows, requests, heads_here, HD
    )
    all_queries = lax.all_gather(queries, "row", axis=0, tiled=True)
    query_count = all_queries.shape[0]
    query_heads = all_queries.reshape(query_count, requests, heads_here, HD)
    query_pos = jnp.arange(query_count, dtype=jnp.int32)
    offset_rows = jnp.arange(block_rows, dtype=jnp.int32)
    in_cache = offset_rows < cache_rows
    cache_pos = row_index * cache_rows + offset_rows
    new_pos = row_index * rows_here + offset_rows - cache_rows
    cache_ok = in_cache[None, :] & (cache_pos[None, :] < cached_len[:, None])
    new_ok = jnp.logical_not(in_cache)[None, :] & (new_pos[None, :] <= query_pos[:, None])
    allowed = cache_ok[:, None, None, :] | new_ok[None, None, :, :]
    scores = (
        jnp.einsum("irhd,jrhd->rhij", query_heads, keys_here, preferred_element_type=jnp.float32)
        * score_scale
    )
    masked = jnp.where(allowed, scores, -1e30)
    block_max = jnp.max(masked, axis=-1)
    weights_now = jnp.where(allowed, jnp.exp(masked - block_max[..., None]), 0.0)
    block_sum = jnp.sum(weights_now, axis=-1)
    product = jnp.einsum(
        "rhij,jrhd->irhd",
        weights_now.astype(jnp.bfloat16),
        values_here,
        preferred_element_type=jnp.float32,
    ).astype(jnp.bfloat16)
    stats = jnp.stack([block_max, block_sum], axis=-1).transpose(2, 0, 1, 3)
    product_back = lax.all_to_all(
        product.reshape(row_count, rows_here, requests, heads_here, HD), "row", 0, 0, tiled=True
    )
    stats_back = lax.all_to_all(
        stats.reshape(row_count, rows_here, requests, heads_here, 2), "row", 0, 0, tiled=True
    )
    part_max = stats_back[..., 0]
    row_top = jnp.max(part_max, axis=0)
    rescale = jnp.exp(part_max - row_top[None])
    row_total = jnp.sum(rescale * stats_back[..., 1], axis=0)
    summed = jnp.sum(rescale[..., None] * product_back.astype(jnp.float32), axis=0)
    attended = (summed / row_total[..., None]).astype(jnp.bfloat16)
    head_weights = out_weight.reshape(heads_here, HD, model_width)
    attn_part = jnp.einsum(
        "irhd,hde->ire", attended, head_weights, preferred_element_type=jnp.float32
    )
    attn_full = lax.psum(attn_part.astype(jnp.bfloat16), "col").astype(jnp.float32)
    mixed_full = (residual.astype(jnp.float32) + attn_full).astype(jnp.bfloat16)
    mixed_f32 = mixed_full.astype(jnp.float32)
    normed = (
        mixed_f32
        * lax.rsqrt(jnp.mean(mixed_f32 * mixed_f32, axis=-1, keepdims=True) + 1e-06)
        * norm_gain
    ).astype(jnp.bfloat16)
    token_count = rows_here * requests
    tokens = normed.reshape(token_count, model_width)
    col_index = lax.axis_index("col")
    col_count = lax.axis_size("col")
    entries_here = w_gate.shape[0]
    experts_dev = max(1, entries_here // GROUPS)
    groups_dev = entries_here // experts_dev
    experts_per_row = col_count * entries_here // GROUPS
    slots = row_count * experts_dev * CAP
    chosen = expert_ids.reshape(token_count * TOPK)
    onehot = (chosen[:, None] == jnp.arange(E, dtype=jnp.int32)[None, :]).astype(jnp.int32)
    slot_index = jnp.sum(jnp.cumsum(onehot, axis=0) * onehot, axis=1) - 1
    dest_row = chosen // experts_per_row
    local_expert = chosen - (dest_row * col_count + col_index) * entries_here // GROUPS
    valid = (local_expert >= 0) & (local_expert < experts_dev)
    place = (dest_row * experts_dev + local_expert) * CAP + slot_index
    place = jnp.where(valid, place, -1).reshape(token_count, TOPK)
    hit = place[:, :, None] == jnp.arange(slots, dtype=jnp.int32)[None, None, :]
    dispatch = jnp.sum(hit.astype(jnp.float32), axis=1).astype(jnp.bfloat16)
    combine = jnp.sum(
        jnp.where(hit, gate_values.reshape(token_count, TOPK, 1), 0.0), axis=1
    )
    outgoing = lax.dot_general(
        dispatch, tokens, (((0,), (0,)), ((), ())), preferred_element_type=jnp.float32
    ).astype(jnp.bfloat16)
    outgoing = outgoing.reshape(row_count, experts_dev, CAP, model_width)
    arrived = lax.all_to_all(outgoing, "row", 0, 0, tiled=True)
    hidden = w_gate.shape[2]
    wg = w_gate.reshape(experts_dev, groups_dev, model_width, hidden)
    wu = w_up.reshape(experts_dev, groups_dev, model_width, hidden)
    wd = w_down.reshape(experts_dev, groups_dev, hidden, model_width)
    gate_proj = jnp.einsum("nlsd,lgdf->lgnsf", arrived, wg, preferred_element_type=jnp.float32)
    up_proj = jnp.einsum("nlsd,lgdf->lgnsf", arrived, wu, preferred_element_type=jnp.float32)
    hidden_act = (jax.nn.silu(gate_proj) * up_proj).astype(jnp.bfloat16)
    expert_out = jnp.einsum(
        "lgnsf,lgfd->nlsd", hidden_act, wd, preferred_element_type=jnp.float32
    ).astype(jnp.bfloat16)
    returned = lax.all_to_all(expert_out, "row", 0, 0, tiled=True).reshape(slots, model_width)
    combine_hi = combine.astype(jnp.bfloat16)
    combine_lo = (combine - combine_hi.astype(jnp.float32)).astype(jnp.bfloat16)
    routed = jnp.dot(combine_hi, returned, preferred_element_type=jnp.float32) + jnp.dot(
        combine_lo, returned, preferred_element_type=jnp.float32
    )
    shared_g = jnp.dot(tokens, shared_gate, preferred_element_type=jnp.float32)
    shared_u = jnp.dot(tokens, shared_up, preferred_element_type=jnp.float32)
    shared_act = (jax.nn.silu(shared_g) * shared_u).astype(jnp.bfloat16)
    shared_part = jnp.dot(shared_act, shared_down, preferred_element_type=jnp.float32)
    ffn_total = lax.psum_scatter(
        (routed + shared_part).astype(jnp.bfloat16), "col", scatter_dimension=1, tiled=True
    )
    col_width = model_width // col_count
    ffn_here = ffn_total.reshape(rows_here, requests, col_width)
    mixed_here = lax.dynamic_slice_in_dim(mixed_full, col_index * col_width, col_width, 2)
    return (mixed_here, ffn_here)


def solution(mesh):
    in_specs = (
        P("row", None, "col"),
        P("row", None, "col"),
        P("row", None, "col"),
        P("row", None, "col"),
        P("row", None, "col"),
        P(),
        P("row", None, None),
        P("col", None),
        P(),
        P("row", None, None),
        P("row", None, None),
        P(("row", "col"), None, None),
        P(("row", "col"), None, None),
        P(("row", "col"), None, None),
        P(None, "col"),
        P(None, "col"),
        P("col", None),
    )
    out_specs = (P("row", None, "col"), P("row", None, "col"))
    return jax.shard_map(body, mesh=mesh, in_specs=in_specs, out_specs=out_specs, check_vma=False)
```

```python
import math

import jax
import jax.numpy as jnp
from jax import lax
from jax.sharding import PartitionSpec as P

HD = 128
E = 64
TOPK = 6
GROUPS = 4
CAP = 24


def body(
    queries,
    new_keys,
    new_values,
    cache_keys,
    cache_values,
    cached_len,
    residual,
    out_weight,
    norm_gain,
    expert_ids,
    gate_values,
    w_gate,
    w_up,
    w_down,
    shared_gate,
    shared_up,
    shared_down,
):
    rows_here = queries.shape[0]
    requests = queries.shape[1]
    heads_here = queries.shape[2] // HD
    cache_rows = cache_keys.shape[0]
    block_rows = cache_rows + rows_here
    model_width = residual.shape[2]
    row_index = lax.axis_index("row")
    row_count = lax.axis_size("row")
    score_scale = 1.0 / math.sqrt(HD)
    keys_here = jnp.concatenate([cache_keys, new_keys], axis=0).reshape(
        block_rows, requests, heads_here, HD
    )
    values_here = jnp.concatenate([cache_values, new_values], axis=0).reshape(
        block_rows, requests, heads_here, HD
    )
    all_queries = lax.all_to_all(
        jnp.broadcast_to(queries[None], (row_count,) + queries.shape), "row", 0, 0, tiled=True
    )
    query_count = row_count * rows_here
    query_heads = all_queries.reshape(query_count, requests, heads_here, HD)
    query_pos = jnp.arange(query_count, dtype=jnp.int32)
    offset_rows = jnp.arange(block_rows, dtype=jnp.int32)
    in_cache = offset_rows < cache_rows
    cache_pos = row_index * cache_rows + offset_rows
    new_pos = row_index * rows_here + offset_rows - cache_rows
    cache_ok = in_cache[None, :] & (cache_pos[None, :] < cached_len[:, None])
    new_ok = jnp.logical_not(in_cache)[None, :] & (new_pos[None, :] <= query_pos[:, None])
    allowed = cache_ok[:, None, None, :] | new_ok[None, None, :, :]
    scores = (
        jnp.einsum("irhd,jrhd->rhij", query_heads, keys_here, preferred_element_type=jnp.float32)
        * score_scale
    )
    masked = jnp.where(allowed, scores, -1e30)
    block_max = jnp.max(masked, axis=-1)
    weights_now = jnp.where(allowed, jnp.exp(masked - block_max[..., None]), 0.0)
    block_sum = jnp.sum(weights_now, axis=-1)
    product = jnp.einsum(
        "rhij,jrhd->irhd",
        weights_now.astype(jnp.bfloat16),
        values_here,
        preferred_element_type=jnp.float32,
    ).astype(jnp.bfloat16)
    stats = jnp.stack([block_max, block_sum], axis=-1).transpose(2, 0, 1, 3)
    product_back = lax.all_to_all(
        product.reshape(row_count, rows_here, requests, heads_here, HD), "row", 0, 0, tiled=True
    )
    stats_back = lax.all_to_all(
        stats.reshape(row_count, rows_here, requests, heads_here, 2), "row", 0, 0, tiled=True
    )
    part_max = stats_back[..., 0]
    row_top = jnp.max(part_max, axis=0)
    rescale = jnp.exp(part_max - row_top[None])
    row_total = jnp.sum(rescale * stats_back[..., 1], axis=0)
    summed = jnp.sum(rescale[..., None] * product_back.astype(jnp.float32), axis=0)
    attended = (summed / row_total[..., None]).astype(jnp.bfloat16)
    head_weights = out_weight.reshape(heads_here, HD, model_width)
    attn_part = jnp.einsum(
        "irhd,hde->ire", attended, head_weights, preferred_element_type=jnp.float32
    )
    col_index = lax.axis_index("col")
    col_count = lax.axis_size("col")
    col_width = model_width // col_count
    token_count = rows_here * requests
    attn_chunks = (
        attn_part.astype(jnp.bfloat16)
        .reshape(token_count, col_count, col_width)
        .transpose(1, 0, 2)
    )
    attn_summed = jnp.sum(
        lax.all_to_all(attn_chunks, "col", 0, 0, tiled=True).astype(jnp.float32), axis=0
    )
    residual_here = lax.dynamic_slice_in_dim(
        residual.reshape(token_count, model_width), col_index * col_width, col_width, 1
    )
    mixed_slice = (residual_here.astype(jnp.float32) + attn_summed).astype(jnp.bfloat16)
    mixed_gathered = lax.all_to_all(
        jnp.broadcast_to(mixed_slice[None], (col_count, token_count, col_width)),
        "col",
        0,
        0,
        tiled=True,
    )
    mixed_full = mixed_gathered.transpose(1, 0, 2).reshape(token_count, model_width)
    mixed_f32 = mixed_full.astype(jnp.float32)
    normed = (
        mixed_f32
        * lax.rsqrt(jnp.mean(mixed_f32 * mixed_f32, axis=-1, keepdims=True) + 1e-06)
        * norm_gain
    ).astype(jnp.bfloat16)
    tokens = normed
    entries_here = w_gate.shape[0]
    experts_dev = max(1, entries_here // GROUPS)
    groups_dev = entries_here // experts_dev
    experts_per_row = col_count * entries_here // GROUPS
    slots = row_count * experts_dev * CAP
    chosen = expert_ids.reshape(token_count * TOPK)
    onehot = (chosen[:, None] == jnp.arange(E, dtype=jnp.int32)[None, :]).astype(jnp.int32)
    slot_index = jnp.sum(jnp.cumsum(onehot, axis=0) * onehot, axis=1) - 1
    dest_row = chosen // experts_per_row
    local_expert = chosen - (dest_row * col_count + col_index) * entries_here // GROUPS
    valid = (local_expert >= 0) & (local_expert < experts_dev)
    place = (dest_row * experts_dev + local_expert) * CAP + slot_index
    place = jnp.where(valid, place, -1).reshape(token_count, TOPK)
    hit = place[:, :, None] == jnp.arange(slots, dtype=jnp.int32)[None, None, :]
    dispatch = jnp.sum(hit.astype(jnp.float32), axis=1).astype(jnp.bfloat16)
    combine = jnp.sum(
        jnp.where(hit, gate_values.reshape(token_count, TOPK, 1), 0.0), axis=1
    )
    outgoing = lax.dot_general(
        dispatch, tokens, (((0,), (0,)), ((), ())), preferred_element_type=jnp.float32
    ).astype(jnp.bfloat16)
    outgoing = outgoing.reshape(row_count, experts_dev, CAP, model_width)
    arrived = lax.all_to_all(outgoing, "row", 0, 0, tiled=True)
    hidden = w_gate.shape[2]
    wg = w_gate.reshape(experts_dev, groups_dev, model_width, hidden)
    wu = w_up.reshape(experts_dev, groups_dev, model_width, hidden)
    wd = w_down.reshape(experts_dev, groups_dev, hidden, model_width)
    gate_proj = jnp.einsum("nlsd,lgdf->lgnsf", arrived, wg, preferred_element_type=jnp.float32)
    up_proj = jnp.einsum("nlsd,lgdf->lgnsf", arrived, wu, preferred_element_type=jnp.float32)
    hidden_act = (jax.nn.silu(gate_proj) * up_proj).astype(jnp.bfloat16)
    expert_out = jnp.einsum(
        "lgnsf,lgfd->nlsd", hidden_act, wd, preferred_element_type=jnp.float32
    ).astype(jnp.bfloat16)
    returned = lax.all_to_all(expert_out, "row", 0, 0, tiled=True).reshape(slots, model_width)
    combine_hi = combine.astype(jnp.bfloat16)
    combine_lo = (combine - combine_hi.astype(jnp.float32)).astype(jnp.bfloat16)
    routed = jnp.dot(combine_hi, returned, preferred_element_type=jnp.float32) + jnp.dot(
        combine_lo, returned, preferred_element_type=jnp.float32
    )
    shared_g = jnp.dot(tokens, shared_gate, preferred_element_type=jnp.float32)
    shared_u = jnp.dot(tokens, shared_up, preferred_element_type=jnp.float32)
    shared_act = (jax.nn.silu(shared_g) * shared_u).astype(jnp.bfloat16)
    shared_part = jnp.dot(shared_act, shared_down, preferred_element_type=jnp.float32)
    ffn_chunks = (
        (routed + shared_part)
        .astype(jnp.bfloat16)
        .reshape(token_count, col_count, col_width)
        .transpose(1, 0, 2)
    )
    ffn_total = jnp.sum(
        lax.all_to_all(ffn_chunks, "col", 0, 0, tiled=True).astype(jnp.float32), axis=0
    )
    ffn_here = ffn_total.astype(jnp.bfloat16).reshape(rows_here, requests, col_width)
    mixed_here = mixed_slice.reshape(rows_here, requests, col_width)
    return (mixed_here, ffn_here)


def solution(mesh):
    in_specs = (
        P("row", None, "col"),
        P("row", None, "col"),
        P("row", None, "col"),
        P("row", None, "col"),
        P("row", None, "col"),
        P(),
        P("row", None, None),
        P("col", None),
        P(),
        P("row", None, None),
        P("row", None, None),
        P(("row", "col"), None, None),
        P(("row", "col"), None, None),
        P(("row", "col"), None, None),
        P(None, "col"),
        P(None, "col"),
        P("col", None),
    )
    out_specs = (P("row", None, "col"), P("row", None, "col"))
    return jax.shard_map(body, mesh=mesh, in_specs=in_specs, out_specs=out_specs, check_vma=False)
```

```python
import math

import jax
import jax.numpy as jnp
from jax import lax
from jax.sharding import PartitionSpec as P

HD = 128
E = 64
TOPK = 6
GROUPS = 4
CAP = 24


def body(
    queries,
    new_keys,
    new_values,
    cache_keys,
    cache_values,
    cached_len,
    residual,
    out_weight,
    norm_gain,
    expert_ids,
    gate_values,
    w_gate,
    w_up,
    w_down,
    shared_gate,
    shared_up,
    shared_down,
):
    rows_here = queries.shape[0]
    requests = queries.shape[1]
    heads_here = queries.shape[2] // HD
    cache_rows = cache_keys.shape[0]
    block_rows = cache_rows + rows_here
    model_width = residual.shape[2]
    row_index = lax.axis_index("row")
    row_count = lax.axis_size("row")
    score_scale = 1.0 / math.sqrt(HD)
    keys_here = jnp.concatenate([cache_keys, new_keys], axis=0).reshape(
        block_rows, requests, heads_here, HD
    )
    values_here = jnp.concatenate([cache_values, new_values], axis=0).reshape(
        block_rows, requests, heads_here, HD
    )
    all_queries = lax.all_to_all(
        jnp.broadcast_to(queries[None], (row_count,) + queries.shape), "row", 0, 0, tiled=True
    )
    query_count = row_count * rows_here
    query_heads = all_queries.reshape(query_count, requests, heads_here, HD)
    query_pos = jnp.arange(query_count, dtype=jnp.int32)
    offset_rows = jnp.arange(block_rows, dtype=jnp.int32)
    in_cache = offset_rows < cache_rows
    cache_pos = row_index * cache_rows + offset_rows
    new_pos = row_index * rows_here + offset_rows - cache_rows
    cache_ok = in_cache[None, :] & (cache_pos[None, :] < cached_len[:, None])
    new_ok = jnp.logical_not(in_cache)[None, :] & (new_pos[None, :] <= query_pos[:, None])
    allowed = cache_ok[:, None, None, :] | new_ok[None, None, :, :]
    scores = (
        jnp.einsum("irhd,jrhd->rhij", query_heads, keys_here, preferred_element_type=jnp.float32)
        * score_scale
    )
    masked = jnp.where(allowed, scores, -1e30)
    block_max = jnp.max(masked, axis=-1)
    weights_now = jnp.where(allowed, jnp.exp(masked - block_max[..., None]), 0.0)
    block_sum = jnp.sum(weights_now, axis=-1)
    product = jnp.einsum(
        "rhij,jrhd->irhd",
        weights_now.astype(jnp.bfloat16),
        values_here,
        preferred_element_type=jnp.float32,
    ).astype(jnp.bfloat16)
    stats = jnp.stack([block_max, block_sum], axis=-1).transpose(2, 0, 1, 3)
    product_back = lax.all_to_all(
        product.reshape(row_count, rows_here, requests, heads_here, HD), "row", 0, 0, tiled=True
    )
    stats_back = lax.all_to_all(
        stats.reshape(row_count, rows_here, requests, heads_here, 2), "row", 0, 0, tiled=True
    )
    part_max = stats_back[..., 0]
    row_top = jnp.max(part_max, axis=0)
    rescale = jnp.exp(part_max - row_top[None])
    row_total = jnp.sum(rescale * stats_back[..., 1], axis=0)
    summed = jnp.sum(rescale[..., None] * product_back.astype(jnp.float32), axis=0)
    attended = (summed / row_total[..., None]).astype(jnp.bfloat16)
    head_weights = out_weight.reshape(heads_here, HD, model_width)
    attn_part = jnp.einsum(
        "irhd,hde->ire", attended, head_weights, preferred_element_type=jnp.float32
    )
    col_index = lax.axis_index("col")
    col_count = lax.axis_size("col")
    col_width = model_width // col_count
    token_count = rows_here * requests
    attn_chunks = (
        attn_part.astype(jnp.bfloat16)
        .reshape(token_count, col_count, col_width)
        .transpose(1, 0, 2)
    )
    attn_summed = jnp.sum(
        lax.all_to_all(attn_chunks, "col", 0, 0, tiled=True).astype(jnp.float32), axis=0
    )
    residual_here = lax.dynamic_slice_in_dim(
        residual.reshape(token_count, model_width), col_index * col_width, col_width, 1
    )
    mixed_slice = (residual_here.astype(jnp.float32) + attn_summed).astype(jnp.bfloat16)
    mixed_gathered = lax.all_to_all(
        jnp.broadcast_to(mixed_slice[None], (col_count, token_count, col_width)),
        "col",
        0,
        0,
        tiled=True,
    )
    mixed_full = mixed_gathered.transpose(1, 0, 2).reshape(token_count, model_width)
    mixed_f32 = mixed_full.astype(jnp.float32)
    normed = (
        mixed_f32
        * lax.rsqrt(jnp.mean(mixed_f32 * mixed_f32, axis=-1, keepdims=True) + 1e-06)
        * norm_gain
    ).astype(jnp.bfloat16)
    tokens = normed
    shared_g = jnp.dot(tokens, shared_gate, preferred_element_type=jnp.float32)
    shared_u = jnp.dot(tokens, shared_up, preferred_element_type=jnp.float32)
    shared_act = (jax.nn.silu(shared_g) * shared_u).astype(jnp.bfloat16)
    shared_part = jnp.dot(shared_act, shared_down, preferred_element_type=jnp.float32)
    shared_chunks = (
        shared_part.astype(jnp.bfloat16).reshape(token_count, col_count, col_width).transpose(1, 0, 2)
    )
    shared_here = jnp.sum(
        lax.all_to_all(shared_chunks, "col", 0, 0, tiled=True).astype(jnp.float32), axis=0
    )
    entries_here = w_gate.shape[0]
    experts_dev = max(1, entries_here // GROUPS)
    groups_dev = entries_here // experts_dev
    devs_per_expert = max(1, GROUPS // entries_here)
    experts_per_row = col_count * entries_here // GROUPS
    device_count = row_count * col_count
    send_slots = row_count * experts_dev * CAP
    all_slots = device_count * experts_dev * CAP
    chosen = expert_ids.reshape(token_count * TOPK)
    onehot = (chosen[:, None] == jnp.arange(E, dtype=jnp.int32)[None, :]).astype(jnp.int32)
    slot_index = jnp.sum(jnp.cumsum(onehot, axis=0) * onehot, axis=1) - 1
    dest_row = chosen // experts_per_row
    local_expert = chosen - (dest_row * col_count + col_index) * entries_here // GROUPS
    valid = (local_expert >= 0) & (local_expert < experts_dev)
    place = (dest_row * experts_dev + local_expert) * CAP + slot_index
    place = jnp.where(valid, place, -1).reshape(token_count, TOPK)
    hit = place[:, :, None] == jnp.arange(send_slots, dtype=jnp.int32)[None, None, :]
    dispatch = jnp.sum(hit.astype(jnp.float32), axis=1).astype(jnp.bfloat16)
    first_device = chosen * GROUPS // entries_here
    combine = jnp.zeros((token_count, all_slots), jnp.float32)
    slot_ids = jnp.arange(all_slots, dtype=jnp.int32)[None, None, :]
    gates = gate_values.reshape(token_count, TOPK, 1)
    for part in range(devs_per_expert):
        device = first_device + part
        owner_expert = chosen - device * entries_here // GROUPS
        spot = ((device * experts_dev + owner_expert) * CAP + slot_index).reshape(token_count, TOPK)
        combine = combine + jnp.sum(jnp.where(spot[:, :, None] == slot_ids, gates, 0.0), axis=1)
    outgoing = lax.dot_general(
        dispatch, tokens, (((0,), (0,)), ((), ())), preferred_element_type=jnp.float32
    ).astype(jnp.bfloat16)
    outgoing = outgoing.reshape(row_count, experts_dev, CAP, model_width)
    arrived = lax.all_to_all(outgoing, "row", 0, 0, tiled=True)
    hidden = w_gate.shape[2]
    wg = w_gate.reshape(experts_dev, groups_dev, model_width, hidden)
    wu = w_up.reshape(experts_dev, groups_dev, model_width, hidden)
    wd = w_down.reshape(experts_dev, groups_dev, hidden, col_count, col_width)
    gate_proj = jnp.einsum("nlsd,lgdf->lgnsf", arrived, wg, preferred_element_type=jnp.float32)
    up_proj = jnp.einsum("nlsd,lgdf->lgnsf", arrived, wu, preferred_element_type=jnp.float32)
    hidden_act = (jax.nn.silu(gate_proj) * up_proj).astype(jnp.bfloat16)
    expert_out = jnp.einsum(
        "lgnsf,lgfcw->nclsw", hidden_act, wd, preferred_element_type=jnp.float32
    ).astype(jnp.bfloat16)
    returned = lax.all_to_all(
        expert_out.reshape(device_count, experts_dev, CAP, col_width),
        ("row", "col"),
        0,
        0,
        tiled=True,
    ).reshape(all_slots, col_width)
    combine_hi = combine.astype(jnp.bfloat16)
    combine_lo = (combine - combine_hi.astype(jnp.float32)).astype(jnp.bfloat16)
    routed = jnp.dot(combine_hi, returned, preferred_element_type=jnp.float32) + jnp.dot(
        combine_lo, returned, preferred_element_type=jnp.float32
    )
    ffn_here = (routed + shared_here).astype(jnp.bfloat16).reshape(rows_here, requests, col_width)
    mixed_here = mixed_slice.reshape(rows_here, requests, col_width)
    return (mixed_here, ffn_here)


def solution(mesh):
    in_specs = (
        P("row", None, "col"),
        P("row", None, "col"),
        P("row", None, "col"),
        P("row", None, "col"),
        P("row", None, "col"),
        P(),
        P("row", None, None),
        P("col", None),
        P(),
        P("row", None, None),
        P("row", None, None),
        P(("row", "col"), None, None),
        P(("row", "col"), None, None),
        P(("row", "col"), None, None),
        P(None, "col"),
        P(None, "col"),
        P("col", None),
    )
    out_specs = (P("row", None, "col"), P("row", None, "col"))
    return jax.shard_map(body, mesh=mesh, in_specs=in_specs, out_specs=out_specs, check_vma=False)
```

```python
import math

import jax
import jax.numpy as jnp
from jax import lax
from jax.sharding import PartitionSpec as P

HD = 128
E = 64
TOPK = 6
GROUPS = 4
CAP = 24


def body(
    queries,
    new_keys,
    new_values,
    cache_keys,
    cache_values,
    cached_len,
    residual,
    out_weight,
    norm_gain,
    expert_ids,
    gate_values,
    w_gate,
    w_up,
    w_down,
    shared_gate,
    shared_up,
    shared_down,
):
    rows_here = queries.shape[0]
    requests = queries.shape[1]
    heads_here = queries.shape[2] // HD
    cache_rows = cache_keys.shape[0]
    block_rows = cache_rows + rows_here
    model_width = residual.shape[2]
    row_index = lax.axis_index("row")
    row_count = lax.axis_size("row")
    score_scale = 1.0 / math.sqrt(HD)
    keys_here = jnp.concatenate([cache_keys, new_keys], axis=0).reshape(
        block_rows, requests, heads_here, HD
    )
    values_here = jnp.concatenate([cache_values, new_values], axis=0).reshape(
        block_rows, requests, heads_here, HD
    )
    all_queries = lax.all_to_all(
        jnp.broadcast_to(queries[None], (row_count,) + queries.shape), "row", 0, 0, tiled=True
    )
    query_count = row_count * rows_here
    query_heads = all_queries.reshape(query_count, requests, heads_here, HD)
    query_pos = jnp.arange(query_count, dtype=jnp.int32)
    offset_rows = jnp.arange(block_rows, dtype=jnp.int32)
    in_cache = offset_rows < cache_rows
    cache_pos = row_index * cache_rows + offset_rows
    new_pos = row_index * rows_here + offset_rows - cache_rows
    cache_ok = in_cache[None, :] & (cache_pos[None, :] < cached_len[:, None])
    new_ok = jnp.logical_not(in_cache)[None, :] & (new_pos[None, :] <= query_pos[:, None])
    allowed = cache_ok[:, None, None, :] | new_ok[None, None, :, :]
    scores = (
        jnp.einsum("irhd,jrhd->rhij", query_heads, keys_here, preferred_element_type=jnp.float32)
        * score_scale
    )
    masked = jnp.where(allowed, scores, -1e30)
    block_max = jnp.max(masked, axis=-1)
    weights_now = jnp.where(allowed, jnp.exp(masked - block_max[..., None]), 0.0)
    block_sum = jnp.sum(weights_now, axis=-1)
    product = jnp.einsum(
        "rhij,jrhd->irhd",
        weights_now.astype(jnp.bfloat16),
        values_here,
        preferred_element_type=jnp.float32,
    ).astype(jnp.bfloat16)
    stats = jnp.stack([block_max, block_sum], axis=-1).transpose(2, 0, 1, 3)
    product_back = lax.all_to_all(
        product.reshape(row_count, rows_here, requests, heads_here, HD), "row", 0, 0, tiled=True
    )
    stats_back = lax.all_to_all(
        stats.reshape(row_count, rows_here, requests, heads_here, 2), "row", 0, 0, tiled=True
    )
    part_max = stats_back[..., 0]
    row_top = jnp.max(part_max, axis=0)
    rescale = jnp.exp(part_max - row_top[None])
    row_total = jnp.sum(rescale * stats_back[..., 1], axis=0)
    summed = jnp.sum(rescale[..., None] * product_back.astype(jnp.float32), axis=0)
    attended = (summed / row_total[..., None]).astype(jnp.bfloat16)
    head_weights = out_weight.reshape(heads_here, HD, model_width)
    attn_part = jnp.einsum(
        "irhd,hde->ire", attended, head_weights, preferred_element_type=jnp.float32
    )
    col_index = lax.axis_index("col")
    col_count = lax.axis_size("col")
    col_width = model_width // col_count
    token_count = rows_here * requests
    attn_chunks = (
        attn_part.astype(jnp.bfloat16)
        .reshape(token_count, col_count, col_width)
        .transpose(1, 0, 2)
    )
    attn_summed = jnp.sum(
        lax.all_to_all(attn_chunks, "col", 0, 0, tiled=True).astype(jnp.float32), axis=0
    )
    residual_here = lax.dynamic_slice_in_dim(
        residual.reshape(token_count, model_width), col_index * col_width, col_width, 1
    )
    mixed_slice = (residual_here.astype(jnp.float32) + attn_summed).astype(jnp.bfloat16)
    mixed_gathered = lax.all_to_all(
        jnp.broadcast_to(mixed_slice[None], (col_count, token_count, col_width)),
        "col",
        0,
        0,
        tiled=True,
    )
    mixed_full = mixed_gathered.transpose(1, 0, 2).reshape(token_count, model_width)
    mixed_f32 = mixed_full.astype(jnp.float32)
    normed = (
        mixed_f32
        * lax.rsqrt(jnp.mean(mixed_f32 * mixed_f32, axis=-1, keepdims=True) + 1e-06)
        * norm_gain
    ).astype(jnp.bfloat16)
    tokens = normed
    entries_here = w_gate.shape[0]
    experts_dev = max(1, entries_here // GROUPS)
    groups_dev = entries_here // experts_dev
    experts_per_row = col_count * entries_here // GROUPS
    slots = row_count * experts_dev * CAP
    chosen = expert_ids.reshape(token_count * TOPK)
    onehot = (chosen[:, None] == jnp.arange(E, dtype=jnp.int32)[None, :]).astype(jnp.int32)
    slot_index = jnp.sum(jnp.cumsum(onehot, axis=0) * onehot, axis=1) - 1
    dest_row = chosen // experts_per_row
    local_expert = chosen - (dest_row * col_count + col_index) * entries_here // GROUPS
    valid = (local_expert >= 0) & (local_expert < experts_dev)
    place = (local_expert * row_count + dest_row) * CAP + slot_index
    place = jnp.where(valid, place, -1).reshape(token_count, TOPK)
    hit = place[:, :, None] == jnp.arange(slots, dtype=jnp.int32)[None, None, :]
    dispatch = jnp.sum(hit.astype(jnp.float32), axis=1).astype(jnp.bfloat16)
    combine = jnp.sum(
        jnp.where(hit, gate_values.reshape(token_count, TOPK, 1), 0.0), axis=1
    )
    combine_hi = combine.astype(jnp.bfloat16)
    combine_lo = (combine - combine_hi.astype(jnp.float32)).astype(jnp.bfloat16)
    outgoing = lax.dot_general(
        dispatch, tokens, (((0,), (0,)), ((), ())), preferred_element_type=jnp.float32
    ).astype(jnp.bfloat16)
    outgoing = outgoing.reshape(experts_dev, row_count, CAP, model_width)
    hidden = w_gate.shape[2]
    wg = w_gate.reshape(experts_dev, groups_dev, model_width, hidden)
    wu = w_up.reshape(experts_dev, groups_dev, model_width, hidden)
    wd = w_down.reshape(experts_dev, groups_dev, hidden, model_width)
    chunk_slots = row_count * CAP
    routed = jnp.zeros((token_count, model_width), jnp.float32)
    for chunk in range(experts_dev):
        arrived = lax.all_to_all(outgoing[chunk], "row", 0, 0, tiled=True).reshape(
            chunk_slots, model_width
        )
        gate_proj = jnp.einsum(
            "td,gdf->gtf", arrived, wg[chunk], preferred_element_type=jnp.float32
        )
        up_proj = jnp.einsum("td,gdf->gtf", arrived, wu[chunk], preferred_element_type=jnp.float32)
        hidden_act = (jax.nn.silu(gate_proj) * up_proj).astype(jnp.bfloat16)
        expert_out = jnp.einsum(
            "gtf,gfd->td", hidden_act, wd[chunk], preferred_element_type=jnp.float32
        ).astype(jnp.bfloat16)
        returned = lax.all_to_all(
            expert_out.reshape(row_count, CAP, model_width), "row", 0, 0, tiled=True
        ).reshape(chunk_slots, model_width)
        picks = slice(chunk * chunk_slots, (chunk + 1) * chunk_slots)
        routed = routed + (
            jnp.dot(combine_hi[:, picks], returned, preferred_element_type=jnp.float32)
            + jnp.dot(combine_lo[:, picks], returned, preferred_element_type=jnp.float32)
        )
    shared_g = jnp.dot(tokens, shared_gate, preferred_element_type=jnp.float32)
    shared_u = jnp.dot(tokens, shared_up, preferred_element_type=jnp.float32)
    shared_act = (jax.nn.silu(shared_g) * shared_u).astype(jnp.bfloat16)
    shared_part = jnp.dot(shared_act, shared_down, preferred_element_type=jnp.float32)
    ffn_chunks = (
        (routed + shared_part)
        .astype(jnp.bfloat16)
        .reshape(token_count, col_count, col_width)
        .transpose(1, 0, 2)
    )
    ffn_total = jnp.sum(
        lax.all_to_all(ffn_chunks, "col", 0, 0, tiled=True).astype(jnp.float32), axis=0
    )
    ffn_here = ffn_total.astype(jnp.bfloat16).reshape(rows_here, requests, col_width)
    mixed_here = mixed_slice.reshape(rows_here, requests, col_width)
    return (mixed_here, ffn_here)


def solution(mesh):
    in_specs = (
        P("row", None, "col"),
        P("row", None, "col"),
        P("row", None, "col"),
        P("row", None, "col"),
        P("row", None, "col"),
        P(),
        P("row", None, None),
        P("col", None),
        P(),
        P("row", None, None),
        P("row", None, None),
        P(("row", "col"), None, None),
        P(("row", "col"), None, None),
        P(("row", "col"), None, None),
        P(None, "col"),
        P(None, "col"),
        P("col", None),
    )
    out_specs = (P("row", None, "col"), P("row", None, "col"))
    return jax.shard_map(body, mesh=mesh, in_specs=in_specs, out_specs=out_specs, check_vma=False)
```

```python
import math

import jax
import jax.numpy as jnp
from jax import lax
from jax.sharding import PartitionSpec as P

HD = 128
E = 64
TOPK = 6
GROUPS = 4
CAP = 24


def body(
    queries,
    new_keys,
    new_values,
    cache_keys,
    cache_values,
    cached_len,
    residual,
    out_weight,
    norm_gain,
    expert_ids,
    gate_values,
    w_gate,
    w_up,
    w_down,
    shared_gate,
    shared_up,
    shared_down,
):
    rows_here = queries.shape[0]
    requests = queries.shape[1]
    heads_here = queries.shape[2] // HD
    cache_rows = cache_keys.shape[0]
    block_rows = cache_rows + rows_here
    model_width = residual.shape[2]
    row_index = lax.axis_index("row")
    row_count = lax.axis_size("row")
    score_scale = 1.0 / math.sqrt(HD)
    keys_here = jnp.concatenate([cache_keys, new_keys], axis=0).reshape(
        block_rows, requests, heads_here, HD
    )
    values_here = jnp.concatenate([cache_values, new_values], axis=0).reshape(
        block_rows, requests, heads_here, HD
    )
    all_queries = lax.all_to_all(
        jnp.broadcast_to(queries[None], (row_count,) + queries.shape), "row", 0, 0, tiled=True
    )
    query_count = row_count * rows_here
    query_heads = all_queries.reshape(query_count, requests, heads_here, HD)
    query_pos = jnp.arange(query_count, dtype=jnp.int32)
    offset_rows = jnp.arange(block_rows, dtype=jnp.int32)
    in_cache = offset_rows < cache_rows
    cache_pos = row_index * cache_rows + offset_rows
    new_pos = row_index * rows_here + offset_rows - cache_rows
    cache_ok = in_cache[None, :] & (cache_pos[None, :] < cached_len[:, None])
    new_ok = jnp.logical_not(in_cache)[None, :] & (new_pos[None, :] <= query_pos[:, None])
    allowed = cache_ok[:, None, None, :] | new_ok[None, None, :, :]
    scores = (
        jnp.einsum("irhd,jrhd->rhij", query_heads, keys_here, preferred_element_type=jnp.float32)
        * score_scale
    )
    masked = jnp.where(allowed, scores, -1e30)
    block_max = jnp.max(masked, axis=-1)
    weights_now = jnp.where(allowed, jnp.exp(masked - block_max[..., None]), 0.0)
    block_sum = jnp.sum(weights_now, axis=-1)
    product = jnp.einsum(
        "rhij,jrhd->irhd",
        weights_now.astype(jnp.bfloat16),
        values_here,
        preferred_element_type=jnp.float32,
    ).astype(jnp.bfloat16)
    stats = jnp.stack([block_max, block_sum], axis=-1).transpose(2, 0, 1, 3)
    product_back = lax.all_to_all(
        product.reshape(row_count, rows_here, requests, heads_here, HD), "row", 0, 0, tiled=True
    )
    stats_back = lax.all_to_all(
        stats.reshape(row_count, rows_here, requests, heads_here, 2), "row", 0, 0, tiled=True
    )
    part_max = stats_back[..., 0]
    row_top = jnp.max(part_max, axis=0)
    rescale = jnp.exp(part_max - row_top[None])
    row_total = jnp.sum(rescale * stats_back[..., 1], axis=0)
    summed = jnp.sum(rescale[..., None] * product_back.astype(jnp.float32), axis=0)
    attended = (summed / row_total[..., None]).astype(jnp.bfloat16)
    head_weights = out_weight.reshape(heads_here, HD, model_width)
    attn_part = jnp.einsum(
        "irhd,hde->ire", attended, head_weights, preferred_element_type=jnp.float32
    )
    col_index = lax.axis_index("col")
    col_count = lax.axis_size("col")
    col_width = model_width // col_count
    token_count = rows_here * requests
    attn_chunks = (
        attn_part.astype(jnp.bfloat16)
        .reshape(token_count, col_count, col_width)
        .transpose(1, 0, 2)
    )
    attn_summed = jnp.sum(
        lax.all_to_all(attn_chunks, "col", 0, 0, tiled=True).astype(jnp.float32), axis=0
    )
    residual_here = lax.dynamic_slice_in_dim(
        residual.reshape(token_count, model_width), col_index * col_width, col_width, 1
    )
    mixed_slice = (residual_here.astype(jnp.float32) + attn_summed).astype(jnp.bfloat16)
    mixed_gathered = lax.all_to_all(
        jnp.broadcast_to(mixed_slice[None], (col_count, token_count, col_width)),
        "col",
        0,
        0,
        tiled=True,
    )
    mixed_full = mixed_gathered.transpose(1, 0, 2).reshape(token_count, model_width)
    mixed_f32 = mixed_full.astype(jnp.float32)
    normed = (
        mixed_f32
        * lax.rsqrt(jnp.mean(mixed_f32 * mixed_f32, axis=-1, keepdims=True) + 1e-06)
        * norm_gain
    ).astype(jnp.bfloat16)
    tokens = normed
    entries_here = w_gate.shape[0]
    experts_dev = max(1, entries_here // GROUPS)
    groups_dev = entries_here // experts_dev
    experts_per_row = col_count * entries_here // GROUPS
    slots = row_count * experts_dev * CAP
    chosen = expert_ids.reshape(token_count * TOPK)
    onehot = (chosen[:, None] == jnp.arange(E, dtype=jnp.int32)[None, :]).astype(jnp.int32)
    slot_index = jnp.sum(jnp.cumsum(onehot, axis=0) * onehot, axis=1) - 1
    dest_row = chosen // experts_per_row
    local_expert = chosen - (dest_row * col_count + col_index) * entries_here // GROUPS
    valid = (local_expert >= 0) & (local_expert < experts_dev)
    place = (dest_row * experts_dev + local_expert) * CAP + slot_index
    place = jnp.where(valid, place, -1).reshape(token_count, TOPK)
    hit = place[:, :, None] == jnp.arange(slots, dtype=jnp.int32)[None, None, :]
    dispatch = jnp.sum(hit.astype(jnp.float32), axis=1).astype(jnp.bfloat16)
    combine = jnp.sum(
        jnp.where(hit, gate_values.reshape(token_count, TOPK, 1), 0.0), axis=1
    )
    outgoing = lax.dot_general(
        dispatch, tokens, (((0,), (0,)), ((), ())), preferred_element_type=jnp.float32
    ).astype(jnp.bfloat16)
    outgoing = outgoing.reshape(row_count, experts_dev, CAP, model_width)
    arrived = lax.all_to_all(outgoing, "row", 0, 0, tiled=True)
    shared_g = jnp.dot(tokens, shared_gate, preferred_element_type=jnp.float32)
    shared_u = jnp.dot(tokens, shared_up, preferred_element_type=jnp.float32)
    shared_act = (jax.nn.silu(shared_g) * shared_u).astype(jnp.bfloat16)
    shared_part = jnp.dot(shared_act, shared_down, preferred_element_type=jnp.float32)
    arrived, shared_part = lax.optimization_barrier((arrived, shared_part))
    hidden = w_gate.shape[2]
    wg = w_gate.reshape(experts_dev, groups_dev, model_width, hidden)
    wu = w_up.reshape(experts_dev, groups_dev, model_width, hidden)
    wd = w_down.reshape(experts_dev, groups_dev, hidden, model_width)
    gate_proj = jnp.einsum("nlsd,lgdf->lgnsf", arrived, wg, preferred_element_type=jnp.float32)
    up_proj = jnp.einsum("nlsd,lgdf->lgnsf", arrived, wu, preferred_element_type=jnp.float32)
    hidden_act = (jax.nn.silu(gate_proj) * up_proj).astype(jnp.bfloat16)
    expert_out = jnp.einsum(
        "lgnsf,lgfd->nlsd", hidden_act, wd, preferred_element_type=jnp.float32
    ).astype(jnp.bfloat16)
    returned = lax.all_to_all(expert_out, "row", 0, 0, tiled=True).reshape(slots, model_width)
    combine_hi = combine.astype(jnp.bfloat16)
    combine_lo = (combine - combine_hi.astype(jnp.float32)).astype(jnp.bfloat16)
    routed = jnp.dot(combine_hi, returned, preferred_element_type=jnp.float32) + jnp.dot(
        combine_lo, returned, preferred_element_type=jnp.float32
    )
    ffn_chunks = (
        (routed + shared_part)
        .astype(jnp.bfloat16)
        .reshape(token_count, col_count, col_width)
        .transpose(1, 0, 2)
    )
    ffn_total = jnp.sum(
        lax.all_to_all(ffn_chunks, "col", 0, 0, tiled=True).astype(jnp.float32), axis=0
    )
    ffn_here = ffn_total.astype(jnp.bfloat16).reshape(rows_here, requests, col_width)
    mixed_here = mixed_slice.reshape(rows_here, requests, col_width)
    return (mixed_here, ffn_here)


def solution(mesh):
    in_specs = (
        P("row", None, "col"),
        P("row", None, "col"),
        P("row", None, "col"),
        P("row", None, "col"),
        P("row", None, "col"),
        P(),
        P("row", None, None),
        P("col", None),
        P(),
        P("row", None, None),
        P("row", None, None),
        P(("row", "col"), None, None),
        P(("row", "col"), None, None),
        P(("row", "col"), None, None),
        P(None, "col"),
        P(None, "col"),
        P("col", None),
    )
    out_specs = (P("row", None, "col"), P("row", None, "col"))
    return jax.shard_map(body, mesh=mesh, in_specs=in_specs, out_specs=out_specs, check_vma=False)
```

```python
import math

import jax
import jax.numpy as jnp
from jax import lax
from jax.sharding import PartitionSpec as P

HD = 128
E = 64
TOPK = 6
GROUPS = 4
CAP = 24


def body(
    queries,
    new_keys,
    new_values,
    cache_keys,
    cache_values,
    cached_len,
    residual,
    out_weight,
    norm_gain,
    expert_ids,
    gate_values,
    w_gate,
    w_up,
    w_down,
    shared_gate,
    shared_up,
    shared_down,
):
    rows_here = queries.shape[0]
    requests = queries.shape[1]
    heads_here = queries.shape[2] // HD
    cache_rows = cache_keys.shape[0]
    block_rows = cache_rows + rows_here
    model_width = residual.shape[2]
    row_index = lax.axis_index("row")
    row_count = lax.axis_size("row")
    score_scale = 1.0 / math.sqrt(HD)
    keys_here = jnp.concatenate([cache_keys, new_keys], axis=0).reshape(
        block_rows, requests, heads_here, HD
    )
    values_here = jnp.concatenate([cache_values, new_values], axis=0).reshape(
        block_rows, requests, heads_here, HD
    )
    all_queries = lax.all_to_all(
        jnp.broadcast_to(queries[None], (row_count,) + queries.shape), "row", 0, 0, tiled=True
    )
    query_count = row_count * rows_here
    query_heads = all_queries.reshape(query_count, requests, heads_here, HD)
    query_pos = jnp.arange(query_count, dtype=jnp.int32)
    offset_rows = jnp.arange(block_rows, dtype=jnp.int32)
    in_cache = offset_rows < cache_rows
    cache_pos = row_index * cache_rows + offset_rows
    new_pos = row_index * rows_here + offset_rows - cache_rows
    cache_ok = in_cache[None, :] & (cache_pos[None, :] < cached_len[:, None])
    new_ok = jnp.logical_not(in_cache)[None, :] & (new_pos[None, :] <= query_pos[:, None])
    allowed = cache_ok[:, None, None, :] | new_ok[None, None, :, :]
    scores = (
        jnp.einsum("irhd,jrhd->rhij", query_heads, keys_here, preferred_element_type=jnp.float32)
        * score_scale
    )
    masked = jnp.where(allowed, scores, -1e30)
    block_max = jnp.max(masked, axis=-1)
    weights_now = jnp.where(allowed, jnp.exp(masked - block_max[..., None]), 0.0)
    block_sum = jnp.sum(weights_now, axis=-1)
    product = jnp.einsum(
        "rhij,jrhd->irhd",
        weights_now.astype(jnp.bfloat16),
        values_here,
        preferred_element_type=jnp.float32,
    ).astype(jnp.bfloat16)
    stats = jnp.stack([block_max, block_sum], axis=-1).transpose(2, 0, 1, 3)
    product_back = lax.all_to_all(
        product.reshape(row_count, rows_here, requests, heads_here, HD), "row", 0, 0, tiled=True
    )
    stats_back = lax.all_to_all(
        stats.reshape(row_count, rows_here, requests, heads_here, 2), "row", 0, 0, tiled=True
    )
    part_max = stats_back[..., 0]
    row_top = jnp.max(part_max, axis=0)
    rescale = jnp.exp(part_max - row_top[None])
    row_total = jnp.sum(rescale * stats_back[..., 1], axis=0)
    summed = jnp.sum(rescale[..., None] * product_back.astype(jnp.float32), axis=0)
    attended = (summed / row_total[..., None]).astype(jnp.bfloat16)
    head_weights = out_weight.reshape(heads_here, HD, model_width)
    attn_part = jnp.einsum(
        "irhd,hde->ire", attended, head_weights, preferred_element_type=jnp.float32
    )
    col_index = lax.axis_index("col")
    col_count = lax.axis_size("col")
    col_width = model_width // col_count
    token_count = rows_here * requests
    attn_chunks = (
        attn_part.astype(jnp.bfloat16)
        .reshape(token_count, col_count, col_width)
        .transpose(1, 0, 2)
    )
    attn_summed = jnp.sum(
        lax.all_to_all(attn_chunks, "col", 0, 0, tiled=True).astype(jnp.float32), axis=0
    )
    residual_here = lax.dynamic_slice_in_dim(
        residual.reshape(token_count, model_width), col_index * col_width, col_width, 1
    )
    mixed_slice = (residual_here.astype(jnp.float32) + attn_summed).astype(jnp.bfloat16)
    mixed_gathered = lax.all_to_all(
        jnp.broadcast_to(mixed_slice[None], (col_count, token_count, col_width)),
        "col",
        0,
        0,
        tiled=True,
    )
    mixed_full = mixed_gathered.transpose(1, 0, 2).reshape(token_count, model_width)
    mixed_f32 = mixed_full.astype(jnp.float32)
    normed = (
        mixed_f32
        * lax.rsqrt(jnp.mean(mixed_f32 * mixed_f32, axis=-1, keepdims=True) + 1e-06)
        * norm_gain
    ).astype(jnp.bfloat16)
    tokens = normed
    entries_here = w_gate.shape[0]
    experts_dev = max(1, entries_here // GROUPS)
    groups_dev = entries_here // experts_dev
    experts_per_row = col_count * entries_here // GROUPS
    slots = row_count * experts_dev * CAP
    chosen = expert_ids.reshape(token_count * TOPK)
    onehot = (chosen[:, None] == jnp.arange(E, dtype=jnp.int32)[None, :]).astype(jnp.int32)
    slot_index = jnp.sum(jnp.cumsum(onehot, axis=0) * onehot, axis=1) - 1
    dest_row = chosen // experts_per_row
    local_expert = chosen - (dest_row * col_count + col_index) * entries_here // GROUPS
    valid = (local_expert >= 0) & (local_expert < experts_dev)
    place = (dest_row * experts_dev + local_expert) * CAP + slot_index
    place = jnp.where(valid, place, -1).reshape(token_count, TOPK)
    hit = place[:, :, None] == jnp.arange(slots, dtype=jnp.int32)[None, None, :]
    dispatch = jnp.sum(hit.astype(jnp.float32), axis=1).astype(jnp.bfloat16)
    combine = jnp.sum(
        jnp.where(hit, gate_values.reshape(token_count, TOPK, 1), 0.0), axis=1
    )
    outgoing = lax.dot_general(
        dispatch, tokens, (((0,), (0,)), ((), ())), preferred_element_type=jnp.float32
    ).astype(jnp.bfloat16)
    outgoing = outgoing.reshape(row_count, experts_dev, CAP, model_width)
    arrived = lax.all_to_all(outgoing, "row", 0, 0, tiled=True)
    shared_g = jnp.dot(tokens, shared_gate, preferred_element_type=jnp.float32)
    shared_u = jnp.dot(tokens, shared_up, preferred_element_type=jnp.float32)
    shared_act = (jax.nn.silu(shared_g) * shared_u).astype(jnp.bfloat16)
    shared_part = jnp.dot(shared_act, shared_down, preferred_element_type=jnp.float32)
    arrived, shared_part = lax.optimization_barrier((arrived, shared_part))
    hidden = w_gate.shape[2]
    wg = w_gate.reshape(experts_dev, groups_dev, model_width, hidden)
    wu = w_up.reshape(experts_dev, groups_dev, model_width, hidden)
    wd = w_down.reshape(experts_dev, groups_dev, hidden, model_width)
    gate_proj = jnp.einsum("nlsd,lgdf->lgnsf", arrived, wg, preferred_element_type=jnp.float32)
    up_proj = jnp.einsum("nlsd,lgdf->lgnsf", arrived, wu, preferred_element_type=jnp.float32)
    hidden_act = lax.optimization_barrier((jax.nn.silu(gate_proj) * up_proj).astype(jnp.bfloat16))
    expert_out = jnp.einsum(
        "lgnsf,lgfd->nlsd", hidden_act, wd, preferred_element_type=jnp.float32
    ).astype(jnp.bfloat16)
    returned = lax.all_to_all(expert_out, "row", 0, 0, tiled=True).reshape(slots, model_width)
    combine_hi = combine.astype(jnp.bfloat16)
    combine_lo = (combine - combine_hi.astype(jnp.float32)).astype(jnp.bfloat16)
    routed = jnp.dot(combine_hi, returned, preferred_element_type=jnp.float32) + jnp.dot(
        combine_lo, returned, preferred_element_type=jnp.float32
    )
    ffn_chunks = (
        (routed + shared_part)
        .astype(jnp.bfloat16)
        .reshape(token_count, col_count, col_width)
        .transpose(1, 0, 2)
    )
    ffn_total = jnp.sum(
        lax.all_to_all(ffn_chunks, "col", 0, 0, tiled=True).astype(jnp.float32), axis=0
    )
    ffn_here = ffn_total.astype(jnp.bfloat16).reshape(rows_here, requests, col_width)
    mixed_here = mixed_slice.reshape(rows_here, requests, col_width)
    return (mixed_here, ffn_here)


def solution(mesh):
    in_specs = (
        P("row", None, "col"),
        P("row", None, "col"),
        P("row", None, "col"),
        P("row", None, "col"),
        P("row", None, "col"),
        P(),
        P("row", None, None),
        P("col", None),
        P(),
        P("row", None, None),
        P("row", None, None),
        P(("row", "col"), None, None),
        P(("row", "col"), None, None),
        P(("row", "col"), None, None),
        P(None, "col"),
        P(None, "col"),
        P("col", None),
    )
    out_specs = (P("row", None, "col"), P("row", None, "col"))
    return jax.shard_map(body, mesh=mesh, in_specs=in_specs, out_specs=out_specs, check_vma=False)
```

```python
import math

import jax
import jax.numpy as jnp
from jax import lax
from jax.sharding import PartitionSpec as P

HD = 128
E = 64
TOPK = 6
GROUPS = 4
CAP = 24


def body(
    queries,
    new_keys,
    new_values,
    cache_keys,
    cache_values,
    cached_len,
    residual,
    out_weight,
    norm_gain,
    expert_ids,
    gate_values,
    w_gate,
    w_up,
    w_down,
    shared_gate,
    shared_up,
    shared_down,
):
    rows_here = queries.shape[0]
    requests = queries.shape[1]
    heads_here = queries.shape[2] // HD
    cache_rows = cache_keys.shape[0]
    block_rows = cache_rows + rows_here
    model_width = residual.shape[2]
    row_index = lax.axis_index("row")
    row_count = lax.axis_size("row")
    score_scale = 1.0 / math.sqrt(HD)
    key_pad = -(-block_rows // 128) * 128
    width_here = heads_here * HD
    keys_here = jnp.concatenate([cache_keys, new_keys], axis=0)
    values_here = jnp.concatenate([cache_values, new_values], axis=0)
    head_of_lane = jnp.arange(width_here, dtype=jnp.int32) // HD
    head_of_col = jnp.arange(heads_here * key_pad, dtype=jnp.int32) // key_pad
    block_mask = head_of_lane[:, None] == head_of_col[None, :]
    keys_t = jnp.pad(keys_here.transpose(1, 2, 0), ((0, 0), (0, 0), (0, key_pad - block_rows)))
    keys_block = jnp.where(
        block_mask[None], jnp.tile(keys_t, (1, 1, heads_here)), jnp.zeros((), keys_here.dtype)
    )
    values_t = jnp.pad(values_here.transpose(1, 0, 2), ((0, 0), (0, key_pad - block_rows), (0, 0)))
    values_block = jnp.where(
        block_mask.T[None], jnp.tile(values_t, (1, heads_here, 1)), jnp.zeros((), values_here.dtype)
    )
    all_queries = lax.all_to_all(
        jnp.broadcast_to(queries[None], (row_count,) + queries.shape), "row", 0, 0, tiled=True
    )
    query_count = row_count * rows_here
    query_rows = all_queries.reshape(query_count, requests, width_here)
    query_pos = jnp.arange(query_count, dtype=jnp.int32)
    offset_rows = jnp.arange(key_pad, dtype=jnp.int32)
    in_cache = offset_rows < cache_rows
    in_block = offset_rows < block_rows
    cache_pos = row_index * cache_rows + offset_rows
    new_pos = row_index * rows_here + offset_rows - cache_rows
    cache_ok = in_cache[None, :] & (cache_pos[None, :] < cached_len[:, None])
    new_ok = (
        jnp.logical_not(in_cache) & in_block
    )[None, :] & (new_pos[None, :] <= query_pos[:, None])
    allowed = cache_ok[:, None, None, :] | new_ok[None, :, None, :]
    scores = (
        jnp.einsum("irk,rkc->ric", query_rows, keys_block, preferred_element_type=jnp.float32)
        * score_scale
    ).reshape(requests, query_count, heads_here, key_pad)
    masked = jnp.where(allowed, scores, -1e30)
    block_max = jnp.max(masked, axis=-1)
    weights_now = jnp.where(allowed, jnp.exp(masked - block_max[..., None]), 0.0)
    block_sum = jnp.sum(weights_now, axis=-1)
    product = jnp.einsum(
        "ric,rck->irk",
        weights_now.astype(jnp.bfloat16).reshape(requests, query_count, heads_here * key_pad),
        values_block,
        preferred_element_type=jnp.float32,
    ).astype(jnp.bfloat16)
    stats = jnp.stack([block_max, block_sum], axis=-1).transpose(1, 0, 2, 3)
    product_back = lax.all_to_all(
        product.reshape(row_count, rows_here, requests, width_here), "row", 0, 0, tiled=True
    )
    stats_back = lax.all_to_all(
        stats.reshape(row_count, rows_here, requests, heads_here, 2), "row", 0, 0, tiled=True
    )
    part_max = stats_back[..., 0]
    row_top = jnp.max(part_max, axis=0)
    rescale = jnp.exp(part_max - row_top[None])
    row_total = jnp.sum(rescale * stats_back[..., 1], axis=0)
    lane_scale = jnp.broadcast_to(
        rescale[..., None], rescale.shape + (HD,)
    ).reshape(row_count, rows_here, requests, width_here)
    summed = jnp.sum(lane_scale * product_back.astype(jnp.float32), axis=0)
    lane_total = jnp.broadcast_to(row_total[..., None], row_total.shape + (HD,)).reshape(
        rows_here, requests, width_here
    )
    attended = (summed / lane_total).astype(jnp.bfloat16)
    attn_part = jnp.einsum(
        "irk,ke->ire", attended, out_weight, preferred_element_type=jnp.float32
    )
    col_index = lax.axis_index("col")
    col_count = lax.axis_size("col")
    col_width = model_width // col_count
    token_count = rows_here * requests
    attn_chunks = (
        attn_part.astype(jnp.bfloat16)
        .reshape(token_count, col_count, col_width)
        .transpose(1, 0, 2)
    )
    attn_summed = jnp.sum(
        lax.all_to_all(attn_chunks, "col", 0, 0, tiled=True).astype(jnp.float32), axis=0
    )
    residual_here = lax.dynamic_slice_in_dim(
        residual.reshape(token_count, model_width), col_index * col_width, col_width, 1
    )
    mixed_slice = (residual_here.astype(jnp.float32) + attn_summed).astype(jnp.bfloat16)
    mixed_gathered = lax.all_to_all(
        jnp.broadcast_to(mixed_slice[None], (col_count, token_count, col_width)),
        "col",
        0,
        0,
        tiled=True,
    )
    mixed_full = mixed_gathered.transpose(1, 0, 2).reshape(token_count, model_width)
    mixed_f32 = mixed_full.astype(jnp.float32)
    normed = (
        mixed_f32
        * lax.rsqrt(jnp.mean(mixed_f32 * mixed_f32, axis=-1, keepdims=True) + 1e-06)
        * norm_gain
    ).astype(jnp.bfloat16)
    tokens = normed
    entries_here = w_gate.shape[0]
    experts_dev = max(1, entries_here // GROUPS)
    groups_dev = entries_here // experts_dev
    experts_per_row = col_count * entries_here // GROUPS
    slots = row_count * experts_dev * CAP
    chosen = expert_ids.reshape(token_count * TOPK)
    onehot = (chosen[:, None] == jnp.arange(E, dtype=jnp.int32)[None, :]).astype(jnp.int32)
    slot_index = jnp.sum(jnp.cumsum(onehot, axis=0) * onehot, axis=1) - 1
    dest_row = chosen // experts_per_row
    local_expert = chosen - (dest_row * col_count + col_index) * entries_here // GROUPS
    valid = (local_expert >= 0) & (local_expert < experts_dev)
    place = (dest_row * experts_dev + local_expert) * CAP + slot_index
    place = jnp.where(valid, place, -1).reshape(token_count, TOPK)
    hit = place[:, :, None] == jnp.arange(slots, dtype=jnp.int32)[None, None, :]
    dispatch = jnp.sum(hit.astype(jnp.float32), axis=1).astype(jnp.bfloat16)
    combine = jnp.sum(
        jnp.where(hit, gate_values.reshape(token_count, TOPK, 1), 0.0), axis=1
    )
    outgoing = lax.dot_general(
        dispatch, tokens, (((0,), (0,)), ((), ())), preferred_element_type=jnp.float32
    ).astype(jnp.bfloat16)
    outgoing = outgoing.reshape(row_count, experts_dev, CAP, model_width)
    arrived = lax.all_to_all(outgoing, "row", 0, 0, tiled=True)
    shared_g = jnp.dot(tokens, shared_gate, preferred_element_type=jnp.float32)
    shared_u = jnp.dot(tokens, shared_up, preferred_element_type=jnp.float32)
    shared_act = (jax.nn.silu(shared_g) * shared_u).astype(jnp.bfloat16)
    shared_part = jnp.dot(shared_act, shared_down, preferred_element_type=jnp.float32)
    arrived, shared_part = lax.optimization_barrier((arrived, shared_part))
    hidden = w_gate.shape[2]
    wg = w_gate.reshape(experts_dev, groups_dev, model_width, hidden)
    wu = w_up.reshape(experts_dev, groups_dev, model_width, hidden)
    wd = w_down.reshape(experts_dev, groups_dev, hidden, model_width)
    gate_proj = jnp.einsum("nlsd,lgdf->lgnsf", arrived, wg, preferred_element_type=jnp.float32)
    up_proj = jnp.einsum("nlsd,lgdf->lgnsf", arrived, wu, preferred_element_type=jnp.float32)
    hidden_act = lax.optimization_barrier((jax.nn.silu(gate_proj) * up_proj).astype(jnp.bfloat16))
    expert_out = jnp.einsum(
        "lgnsf,lgfd->nlsd", hidden_act, wd, preferred_element_type=jnp.float32
    ).astype(jnp.bfloat16)
    returned = lax.all_to_all(expert_out, "row", 0, 0, tiled=True).reshape(slots, model_width)
    combine_hi = combine.astype(jnp.bfloat16)
    combine_lo = (combine - combine_hi.astype(jnp.float32)).astype(jnp.bfloat16)
    routed = jnp.dot(combine_hi, returned, preferred_element_type=jnp.float32) + jnp.dot(
        combine_lo, returned, preferred_element_type=jnp.float32
    )
    ffn_chunks = (
        (routed + shared_part)
        .astype(jnp.bfloat16)
        .reshape(token_count, col_count, col_width)
        .transpose(1, 0, 2)
    )
    ffn_total = jnp.sum(
        lax.all_to_all(ffn_chunks, "col", 0, 0, tiled=True).astype(jnp.float32), axis=0
    )
    ffn_here = ffn_total.astype(jnp.bfloat16).reshape(rows_here, requests, col_width)
    mixed_here = mixed_slice.reshape(rows_here, requests, col_width)
    return (mixed_here, ffn_here)


def solution(mesh):
    in_specs = (
        P("row", None, "col"),
        P("row", None, "col"),
        P("row", None, "col"),
        P("row", None, "col"),
        P("row", None, "col"),
        P(),
        P("row", None, None),
        P("col", None),
        P(),
        P("row", None, None),
        P("row", None, None),
        P(("row", "col"), None, None),
        P(("row", "col"), None, None),
        P(("row", "col"), None, None),
        P(None, "col"),
        P(None, "col"),
        P("col", None),
    )
    out_specs = (P("row", None, "col"), P("row", None, "col"))
    return jax.shard_map(body, mesh=mesh, in_specs=in_specs, out_specs=out_specs, check_vma=False)
```

```python
import math

import jax
import jax.numpy as jnp
from jax import lax
from jax.sharding import PartitionSpec as P

HD = 128
E = 64
TOPK = 6
GROUPS = 4
CAP = 24


def body(
    queries,
    new_keys,
    new_values,
    cache_keys,
    cache_values,
    cached_len,
    residual,
    out_weight,
    norm_gain,
    expert_ids,
    gate_values,
    w_gate,
    w_up,
    w_down,
    shared_gate,
    shared_up,
    shared_down,
):
    rows_here = queries.shape[0]
    requests = queries.shape[1]
    heads_here = queries.shape[2] // HD
    cache_rows = cache_keys.shape[0]
    block_rows = cache_rows + rows_here
    model_width = residual.shape[2]
    row_index = lax.axis_index("row")
    row_count = lax.axis_size("row")
    score_scale = 1.0 / math.sqrt(HD)
    key_pad = -(-block_rows // 128) * 128
    width_here = heads_here * HD
    keys_here = jnp.concatenate([cache_keys, new_keys], axis=0)
    values_here = jnp.concatenate([cache_values, new_values], axis=0)
    head_of_lane = jnp.arange(width_here, dtype=jnp.int32) // HD
    head_of_col = jnp.arange(heads_here * key_pad, dtype=jnp.int32) // key_pad
    block_mask = head_of_lane[:, None] == head_of_col[None, :]
    keys_t = jnp.pad(keys_here.transpose(1, 2, 0), ((0, 0), (0, 0), (0, key_pad - block_rows)))
    keys_block = jnp.where(
        block_mask[None], jnp.tile(keys_t, (1, 1, heads_here)), jnp.zeros((), keys_here.dtype)
    )
    values_t = jnp.pad(values_here.transpose(1, 0, 2), ((0, 0), (0, key_pad - block_rows), (0, 0)))
    values_block = jnp.where(
        block_mask.T[None], jnp.tile(values_t, (1, heads_here, 1)), jnp.zeros((), values_here.dtype)
    )
    all_queries = lax.all_to_all(
        jnp.broadcast_to(queries[None], (row_count,) + queries.shape), "row", 0, 0, tiled=True
    )
    query_count = row_count * rows_here
    query_rows = all_queries.reshape(query_count, requests, width_here)
    query_pos = jnp.arange(query_count, dtype=jnp.int32)
    offset_rows = jnp.arange(key_pad, dtype=jnp.int32)
    in_cache = offset_rows < cache_rows
    in_block = offset_rows < block_rows
    cache_pos = row_index * cache_rows + offset_rows
    new_pos = row_index * rows_here + offset_rows - cache_rows
    cache_ok = in_cache[None, :] & (cache_pos[None, :] < cached_len[:, None])
    new_ok = (
        jnp.logical_not(in_cache) & in_block
    )[None, :] & (new_pos[None, :] <= query_pos[:, None])
    allowed = cache_ok[:, None, None, :] | new_ok[None, :, None, :]
    scores = (
        jnp.einsum("irk,rkc->ric", query_rows, keys_block, preferred_element_type=jnp.float32)
        * score_scale
    ).reshape(requests, query_count, heads_here, key_pad)
    masked = jnp.where(allowed, scores, -1e30)
    block_max = jnp.max(masked, axis=-1)
    weights_now = jnp.where(allowed, jnp.exp(masked - block_max[..., None]), 0.0)
    block_sum = jnp.sum(weights_now, axis=-1)
    product = jnp.einsum(
        "ric,rck->irk",
        weights_now.astype(jnp.bfloat16).reshape(requests, query_count, heads_here * key_pad),
        values_block,
        preferred_element_type=jnp.float32,
    ).astype(jnp.bfloat16)
    stats = jnp.stack([block_max, block_sum], axis=-1).transpose(1, 0, 2, 3)
    product_back = lax.all_to_all(
        product.reshape(row_count, rows_here, requests, width_here), "row", 0, 0, tiled=True
    )
    stats_back = lax.all_to_all(
        stats.reshape(row_count, rows_here, requests, heads_here, 2), "row", 0, 0, tiled=True
    )
    part_max = stats_back[..., 0]
    row_top = jnp.max(part_max, axis=0)
    rescale = jnp.exp(part_max - row_top[None])
    row_total = jnp.sum(rescale * stats_back[..., 1], axis=0)
    lane_scale = jnp.broadcast_to(
        rescale[..., None], rescale.shape + (HD,)
    ).reshape(row_count, rows_here, requests, width_here)
    summed = jnp.sum(lane_scale * product_back.astype(jnp.float32), axis=0)
    lane_total = jnp.broadcast_to(row_total[..., None], row_total.shape + (HD,)).reshape(
        rows_here, requests, width_here
    )
    attended = (summed / lane_total).astype(jnp.bfloat16)
    col_index = lax.axis_index("col")
    col_count = lax.axis_size("col")
    col_width = model_width // col_count
    token_count = rows_here * requests
    attn_chunks = jnp.einsum(
        "tk,kcw->ctw",
        attended.reshape(token_count, width_here),
        out_weight.reshape(width_here, col_count, col_width),
        preferred_element_type=jnp.float32,
    ).astype(jnp.bfloat16)
    attn_summed = jnp.sum(
        lax.all_to_all(attn_chunks, "col", 0, 0, tiled=True).astype(jnp.float32), axis=0
    )
    residual_here = lax.dynamic_slice_in_dim(
        residual.reshape(token_count, model_width), col_index * col_width, col_width, 1
    )
    mixed_slice = (residual_here.astype(jnp.float32) + attn_summed).astype(jnp.bfloat16)
    mixed_gathered = lax.all_to_all(
        jnp.broadcast_to(mixed_slice[None], (col_count, token_count, col_width)),
        "col",
        0,
        0,
        tiled=True,
    )
    mixed_full = mixed_gathered.transpose(1, 0, 2).reshape(token_count, model_width)
    mixed_f32 = mixed_full.astype(jnp.float32)
    normed = (
        mixed_f32
        * lax.rsqrt(jnp.mean(mixed_f32 * mixed_f32, axis=-1, keepdims=True) + 1e-06)
        * norm_gain
    ).astype(jnp.bfloat16)
    tokens = normed
    entries_here = w_gate.shape[0]
    experts_dev = max(1, entries_here // GROUPS)
    groups_dev = entries_here // experts_dev
    experts_per_row = col_count * entries_here // GROUPS
    slots = row_count * experts_dev * CAP
    chosen = expert_ids.reshape(token_count * TOPK)
    onehot = (chosen[:, None] == jnp.arange(E, dtype=jnp.int32)[None, :]).astype(jnp.int32)
    slot_index = jnp.sum(jnp.cumsum(onehot, axis=0) * onehot, axis=1) - 1
    dest_row = chosen // experts_per_row
    local_expert = chosen - (dest_row * col_count + col_index) * entries_here // GROUPS
    valid = (local_expert >= 0) & (local_expert < experts_dev)
    place = (dest_row * experts_dev + local_expert) * CAP + slot_index
    place = jnp.where(valid, place, -1).reshape(token_count, TOPK)
    hit = place[:, :, None] == jnp.arange(slots, dtype=jnp.int32)[None, None, :]
    dispatch = jnp.sum(hit.astype(jnp.float32), axis=1).astype(jnp.bfloat16)
    combine = jnp.sum(
        jnp.where(hit, gate_values.reshape(token_count, TOPK, 1), 0.0), axis=1
    )
    outgoing = lax.dot_general(
        dispatch, tokens, (((0,), (0,)), ((), ())), preferred_element_type=jnp.float32
    ).astype(jnp.bfloat16)
    outgoing = outgoing.reshape(row_count, experts_dev, CAP, model_width)
    arrived = lax.all_to_all(outgoing, "row", 0, 0, tiled=True)
    shared_g = jnp.dot(tokens, shared_gate, preferred_element_type=jnp.float32)
    shared_u = jnp.dot(tokens, shared_up, preferred_element_type=jnp.float32)
    shared_act = (jax.nn.silu(shared_g) * shared_u).astype(jnp.bfloat16)
    shared_part = jnp.dot(shared_act, shared_down, preferred_element_type=jnp.float32)
    arrived, shared_part = lax.optimization_barrier((arrived, shared_part))
    hidden = w_gate.shape[2]
    wg = w_gate.reshape(experts_dev, groups_dev, model_width, hidden)
    wu = w_up.reshape(experts_dev, groups_dev, model_width, hidden)
    wd = w_down.reshape(experts_dev, groups_dev, hidden, model_width)
    gate_proj = jnp.einsum("nlsd,lgdf->lgnsf", arrived, wg, preferred_element_type=jnp.float32)
    up_proj = jnp.einsum("nlsd,lgdf->lgnsf", arrived, wu, preferred_element_type=jnp.float32)
    hidden_act = lax.optimization_barrier((jax.nn.silu(gate_proj) * up_proj).astype(jnp.bfloat16))
    expert_out = jnp.einsum(
        "lgnsf,lgfd->nlsd", hidden_act, wd, preferred_element_type=jnp.float32
    ).astype(jnp.bfloat16)
    returned = lax.all_to_all(expert_out, "row", 0, 0, tiled=True).reshape(slots, model_width)
    combine_hi = combine.astype(jnp.bfloat16)
    combine_lo = (combine - combine_hi.astype(jnp.float32)).astype(jnp.bfloat16)
    routed = jnp.dot(combine_hi, returned, preferred_element_type=jnp.float32) + jnp.dot(
        combine_lo, returned, preferred_element_type=jnp.float32
    )
    ffn_chunks = (
        (routed + shared_part)
        .astype(jnp.bfloat16)
        .reshape(token_count, col_count, col_width)
        .transpose(1, 0, 2)
    )
    ffn_total = jnp.sum(
        lax.all_to_all(ffn_chunks, "col", 0, 0, tiled=True).astype(jnp.float32), axis=0
    )
    ffn_here = ffn_total.astype(jnp.bfloat16).reshape(rows_here, requests, col_width)
    mixed_here = mixed_slice.reshape(rows_here, requests, col_width)
    return (mixed_here, ffn_here)


def solution(mesh):
    in_specs = (
        P("row", None, "col"),
        P("row", None, "col"),
        P("row", None, "col"),
        P("row", None, "col"),
        P("row", None, "col"),
        P(),
        P("row", None, None),
        P("col", None),
        P(),
        P("row", None, None),
        P("row", None, None),
        P(("row", "col"), None, None),
        P(("row", "col"), None, None),
        P(("row", "col"), None, None),
        P(None, "col"),
        P(None, "col"),
        P("col", None),
    )
    out_specs = (P("row", None, "col"), P("row", None, "col"))
    return jax.shard_map(body, mesh=mesh, in_specs=in_specs, out_specs=out_specs, check_vma=False)
```

```python
import math

import jax
import jax.numpy as jnp
from jax import lax
from jax.sharding import PartitionSpec as P

HD = 128
E = 64
TOPK = 6
GROUPS = 4
CAP = 24


def body(
    queries,
    new_keys,
    new_values,
    cache_keys,
    cache_values,
    cached_len,
    residual,
    out_weight,
    norm_gain,
    expert_ids,
    gate_values,
    w_gate,
    w_up,
    w_down,
    shared_gate,
    shared_up,
    shared_down,
):
    rows_here = queries.shape[0]
    requests = queries.shape[1]
    heads_here = queries.shape[2] // HD
    cache_rows = cache_keys.shape[0]
    block_rows = cache_rows + rows_here
    model_width = residual.shape[2]
    row_index = lax.axis_index("row")
    row_count = lax.axis_size("row")
    score_scale = 1.0 / math.sqrt(HD)
    key_pad = -(-block_rows // 128) * 128
    width_here = heads_here * HD
    keys_here = jnp.concatenate([cache_keys, new_keys], axis=0)
    values_here = jnp.concatenate([cache_values, new_values], axis=0)
    head_of_lane = jnp.arange(width_here, dtype=jnp.int32) // HD
    head_of_col = jnp.arange(heads_here * key_pad, dtype=jnp.int32) // key_pad
    block_mask = head_of_lane[:, None] == head_of_col[None, :]
    keys_t = jnp.pad(keys_here.transpose(1, 2, 0), ((0, 0), (0, 0), (0, key_pad - block_rows)))
    keys_block = jnp.where(
        block_mask[None], jnp.tile(keys_t, (1, 1, heads_here)), jnp.zeros((), keys_here.dtype)
    )
    values_t = jnp.pad(values_here.transpose(1, 0, 2), ((0, 0), (0, key_pad - block_rows), (0, 0)))
    values_block = jnp.where(
        block_mask.T[None], jnp.tile(values_t, (1, heads_here, 1)), jnp.zeros((), values_here.dtype)
    )
    all_queries = lax.all_to_all(
        jnp.broadcast_to(queries[None], (row_count,) + queries.shape), "row", 0, 0, tiled=True
    )
    query_count = row_count * rows_here
    query_rows = all_queries.reshape(query_count, requests, width_here)
    query_pos = jnp.arange(query_count, dtype=jnp.int32)
    offset_rows = jnp.arange(key_pad, dtype=jnp.int32)
    in_cache = offset_rows < cache_rows
    in_block = offset_rows < block_rows
    cache_pos = row_index * cache_rows + offset_rows
    new_pos = row_index * rows_here + offset_rows - cache_rows
    cache_ok = in_cache[None, :] & (cache_pos[None, :] < cached_len[:, None])
    new_ok = (
        jnp.logical_not(in_cache) & in_block
    )[None, :] & (new_pos[None, :] <= query_pos[:, None])
    allowed = cache_ok[:, None, None, :] | new_ok[None, :, None, :]
    scores = (
        jnp.einsum("irk,rkc->ric", query_rows, keys_block, preferred_element_type=jnp.float32)
        * score_scale
    ).reshape(requests, query_count, heads_here, key_pad)
    masked = jnp.where(allowed, scores, -1e30)
    block_max = jnp.max(masked, axis=-1)
    weights_now = jnp.where(allowed, jnp.exp(masked - block_max[..., None]), 0.0)
    block_sum = jnp.sum(weights_now, axis=-1)
    product = jnp.einsum(
        "ric,rck->irk",
        weights_now.astype(jnp.bfloat16).reshape(requests, query_count, heads_here * key_pad),
        values_block,
        preferred_element_type=jnp.float32,
    ).astype(jnp.bfloat16)
    stats = jnp.stack([block_max, block_sum], axis=-1).transpose(1, 0, 2, 3)
    product_back = lax.all_to_all(
        product.reshape(row_count, rows_here, requests, width_here), "row", 0, 0, tiled=True
    )
    stats_back = lax.all_to_all(
        stats.reshape(row_count, rows_here, requests, heads_here, 2), "row", 0, 0, tiled=True
    )
    part_max = stats_back[..., 0]
    row_top = jnp.max(part_max, axis=0)
    rescale = jnp.exp(part_max - row_top[None])
    row_total = jnp.sum(rescale * stats_back[..., 1], axis=0)
    lane_scale = jnp.broadcast_to(
        rescale[..., None], rescale.shape + (HD,)
    ).reshape(row_count, rows_here, requests, width_here)
    summed = jnp.sum(lane_scale * product_back.astype(jnp.float32), axis=0)
    lane_total = jnp.broadcast_to(row_total[..., None], row_total.shape + (HD,)).reshape(
        rows_here, requests, width_here
    )
    attended = (summed / lane_total).astype(jnp.bfloat16)
    col_index = lax.axis_index("col")
    col_count = lax.axis_size("col")
    col_width = model_width // col_count
    token_count = rows_here * requests
    attn_chunks = jnp.einsum(
        "tk,kcw->ctw",
        attended.reshape(token_count, width_here),
        out_weight.reshape(width_here, col_count, col_width),
        preferred_element_type=jnp.float32,
    ).astype(jnp.bfloat16)
    attn_summed = jnp.sum(
        lax.all_to_all(attn_chunks, "col", 0, 0, tiled=True).astype(jnp.float32), axis=0
    )
    residual_here = lax.dynamic_slice_in_dim(
        residual.reshape(token_count, model_width), col_index * col_width, col_width, 1
    )
    mixed_slice = (residual_here.astype(jnp.float32) + attn_summed).astype(jnp.bfloat16)
    mixed_gathered = lax.all_to_all(
        jnp.broadcast_to(mixed_slice[None], (col_count, token_count, col_width)),
        "col",
        0,
        0,
        tiled=True,
    )
    mixed_full = mixed_gathered.transpose(1, 0, 2).reshape(token_count, model_width)
    mixed_f32 = mixed_full.astype(jnp.float32)
    normed = (
        mixed_f32
        * lax.rsqrt(jnp.mean(mixed_f32 * mixed_f32, axis=-1, keepdims=True) + 1e-06)
        * norm_gain
    ).astype(jnp.bfloat16)
    tokens = normed
    entries_here = w_gate.shape[0]
    experts_dev = max(1, entries_here // GROUPS)
    groups_dev = entries_here // experts_dev
    experts_per_row = col_count * entries_here // GROUPS
    slots = row_count * experts_dev * CAP
    chosen = expert_ids.reshape(token_count * TOPK)
    onehot = (chosen[:, None] == jnp.arange(E, dtype=jnp.int32)[None, :]).astype(jnp.int32)
    slot_index = jnp.sum(jnp.cumsum(onehot, axis=0) * onehot, axis=1) - 1
    dest_row = chosen // experts_per_row
    local_expert = chosen - (dest_row * col_count + col_index) * entries_here // GROUPS
    valid = (local_expert >= 0) & (local_expert < experts_dev)
    place = (dest_row * experts_dev + local_expert) * CAP + slot_index
    place = jnp.where(valid, place, -1).reshape(token_count, TOPK)
    hit = place[:, :, None] == jnp.arange(slots, dtype=jnp.int32)[None, None, :]
    dispatch = jnp.sum(hit.astype(jnp.float32), axis=1).astype(jnp.bfloat16)
    combine = jnp.sum(
        jnp.where(hit, gate_values.reshape(token_count, TOPK, 1), 0.0), axis=1
    )
    outgoing = lax.dot_general(
        dispatch, tokens, (((0,), (0,)), ((), ())), preferred_element_type=jnp.float32
    ).astype(jnp.bfloat16)
    outgoing = outgoing.reshape(row_count, experts_dev, CAP, model_width)
    arrived = lax.all_to_all(outgoing, "row", 0, 0, tiled=True)
    shared_g = jnp.dot(tokens, shared_gate, preferred_element_type=jnp.float32)
    shared_u = jnp.dot(tokens, shared_up, preferred_element_type=jnp.float32)
    shared_act = (jax.nn.silu(shared_g) * shared_u).astype(jnp.bfloat16)
    shared_part = jnp.dot(shared_act, shared_down, preferred_element_type=jnp.float32)
    arrived, shared_part = lax.optimization_barrier((arrived, shared_part))
    hidden = w_gate.shape[2]
    wg = w_gate.reshape(experts_dev, groups_dev, model_width, hidden)
    wu = w_up.reshape(experts_dev, groups_dev, model_width, hidden)
    wd = w_down.reshape(experts_dev, groups_dev, hidden, model_width)
    combine_hi = combine.astype(jnp.bfloat16).reshape(token_count, row_count, experts_dev, CAP)
    combine_lo = (combine - combine_hi.reshape(token_count, slots).astype(jnp.float32)).astype(
        jnp.bfloat16
    ).reshape(token_count, row_count, experts_dev, CAP)
    routed = jnp.zeros((token_count, model_width), jnp.float32)
    for chunk in range(experts_dev):
        rows_in = arrived[:, chunk].reshape(row_count * CAP, model_width)
        gate_proj = jnp.einsum(
            "td,gdf->gtf", rows_in, wg[chunk], preferred_element_type=jnp.float32
        )
        up_proj = jnp.einsum("td,gdf->gtf", rows_in, wu[chunk], preferred_element_type=jnp.float32)
        hidden_act = lax.optimization_barrier(
            (jax.nn.silu(gate_proj) * up_proj).astype(jnp.bfloat16)
        )
        expert_out = jnp.einsum(
            "gtf,gfd->td", hidden_act, wd[chunk], preferred_element_type=jnp.float32
        ).astype(jnp.bfloat16)
        returned = lax.all_to_all(
            expert_out.reshape(row_count, CAP, model_width), "row", 0, 0, tiled=True
        ).reshape(row_count * CAP, model_width)
        pick_hi = combine_hi[:, :, chunk].reshape(token_count, row_count * CAP)
        pick_lo = combine_lo[:, :, chunk].reshape(token_count, row_count * CAP)
        routed = routed + (
            jnp.dot(pick_hi, returned, preferred_element_type=jnp.float32)
            + jnp.dot(pick_lo, returned, preferred_element_type=jnp.float32)
        )
    ffn_chunks = (
        (routed + shared_part)
        .astype(jnp.bfloat16)
        .reshape(token_count, col_count, col_width)
        .transpose(1, 0, 2)
    )
    ffn_total = jnp.sum(
        lax.all_to_all(ffn_chunks, "col", 0, 0, tiled=True).astype(jnp.float32), axis=0
    )
    ffn_here = ffn_total.astype(jnp.bfloat16).reshape(rows_here, requests, col_width)
    mixed_here = mixed_slice.reshape(rows_here, requests, col_width)
    return (mixed_here, ffn_here)


def solution(mesh):
    in_specs = (
        P("row", None, "col"),
        P("row", None, "col"),
        P("row", None, "col"),
        P("row", None, "col"),
        P("row", None, "col"),
        P(),
        P("row", None, None),
        P("col", None),
        P(),
        P("row", None, None),
        P("row", None, None),
        P(("row", "col"), None, None),
        P(("row", "col"), None, None),
        P(("row", "col"), None, None),
        P(None, "col"),
        P(None, "col"),
        P("col", None),
    )
    out_specs = (P("row", None, "col"), P("row", None, "col"))
    return jax.shard_map(body, mesh=mesh, in_specs=in_specs, out_specs=out_specs, check_vma=False)
```

```python
import math

import jax
import jax.numpy as jnp
from jax import lax
from jax.sharding import PartitionSpec as P

HD = 128
E = 64
TOPK = 6
GROUPS = 4
CAP = 24


def body(
    queries,
    new_keys,
    new_values,
    cache_keys,
    cache_values,
    cached_len,
    residual,
    out_weight,
    norm_gain,
    expert_ids,
    gate_values,
    w_gate,
    w_up,
    w_down,
    shared_gate,
    shared_up,
    shared_down,
):
    rows_here = queries.shape[0]
    requests = queries.shape[1]
    heads_here = queries.shape[2] // HD
    cache_rows = cache_keys.shape[0]
    block_rows = cache_rows + rows_here
    model_width = residual.shape[2]
    row_index = lax.axis_index("row")
    row_count = lax.axis_size("row")
    score_scale = 1.0 / math.sqrt(HD)
    key_pad = -(-block_rows // 128) * 128
    width_here = heads_here * HD
    keys_here = jnp.concatenate([cache_keys, new_keys], axis=0)
    values_here = jnp.concatenate([cache_values, new_values], axis=0)
    head_of_lane = jnp.arange(width_here, dtype=jnp.int32) // HD
    head_of_col = jnp.arange(heads_here * key_pad, dtype=jnp.int32) // key_pad
    block_mask = head_of_lane[:, None] == head_of_col[None, :]
    keys_t = jnp.pad(keys_here.transpose(1, 2, 0), ((0, 0), (0, 0), (0, key_pad - block_rows)))
    keys_block = jnp.where(
        block_mask[None], jnp.tile(keys_t, (1, 1, heads_here)), jnp.zeros((), keys_here.dtype)
    )
    values_t = jnp.pad(values_here.transpose(1, 0, 2), ((0, 0), (0, key_pad - block_rows), (0, 0)))
    values_block = jnp.where(
        block_mask.T[None], jnp.tile(values_t, (1, heads_here, 1)), jnp.zeros((), values_here.dtype)
    )
    all_queries = lax.all_to_all(
        jnp.broadcast_to(queries[None], (row_count,) + queries.shape), "row", 0, 0, tiled=True
    )
    query_count = row_count * rows_here
    query_rows = all_queries.reshape(query_count, requests, width_here)
    query_pos = jnp.arange(query_count, dtype=jnp.int32)
    offset_rows = jnp.arange(key_pad, dtype=jnp.int32)
    in_cache = offset_rows < cache_rows
    in_block = offset_rows < block_rows
    cache_pos = row_index * cache_rows + offset_rows
    new_pos = row_index * rows_here + offset_rows - cache_rows
    cache_ok = in_cache[None, :] & (cache_pos[None, :] < cached_len[:, None])
    new_ok = (
        jnp.logical_not(in_cache) & in_block
    )[None, :] & (new_pos[None, :] <= query_pos[:, None])
    allowed = cache_ok[:, None, None, :] | new_ok[None, :, None, :]
    scores = (
        jnp.einsum("irk,rkc->ric", query_rows, keys_block, preferred_element_type=jnp.float32)
        * score_scale
    ).reshape(requests, query_count, heads_here, key_pad)
    masked = jnp.where(allowed, scores, -1e30)
    block_max = jnp.max(masked, axis=-1)
    weights_now = jnp.where(allowed, jnp.exp(masked - block_max[..., None]), 0.0)
    block_sum = jnp.sum(weights_now, axis=-1)
    product = jnp.einsum(
        "ric,rck->irk",
        weights_now.astype(jnp.bfloat16).reshape(requests, query_count, heads_here * key_pad),
        values_block,
        preferred_element_type=jnp.float32,
    ).astype(jnp.bfloat16)
    stats = jnp.stack([block_max, block_sum], axis=-1).transpose(1, 0, 2, 3)
    stats_flat = stats.reshape(row_count, rows_here * requests * heads_here * 2)
    stats_hi = lax.reduce_precision(stats_flat, exponent_bits=8, mantissa_bits=7)
    stats_rest = stats_flat - stats_hi
    stats_mid = lax.reduce_precision(stats_rest, exponent_bits=8, mantissa_bits=7)
    stats_lo = stats_rest - stats_mid
    stat_rows = (
        jnp.stack([stats_hi, stats_mid, stats_lo], axis=1)
        .astype(jnp.bfloat16)
        .reshape(row_count, -1, width_here)
    )
    packed = jnp.concatenate(
        [product.reshape(row_count, rows_here * requests, width_here), stat_rows], axis=1
    )
    packed_back = lax.all_to_all(packed, "row", 0, 0, tiled=True)
    product_back = packed_back[:, : rows_here * requests].reshape(
        row_count, rows_here, requests, width_here
    )
    stats_parts = (
        packed_back[:, rows_here * requests :].astype(jnp.float32).reshape(row_count, 3, -1)
    )
    stats_back = (stats_parts[:, 0] + stats_parts[:, 1] + stats_parts[:, 2]).reshape(
        row_count, rows_here, requests, heads_here, 2
    )
    part_max = stats_back[..., 0]
    row_top = jnp.max(part_max, axis=0)
    rescale = jnp.exp(part_max - row_top[None])
    row_total = jnp.sum(rescale * stats_back[..., 1], axis=0)
    lane_scale = jnp.broadcast_to(
        rescale[..., None], rescale.shape + (HD,)
    ).reshape(row_count, rows_here, requests, width_here)
    summed = jnp.sum(lane_scale * product_back.astype(jnp.float32), axis=0)
    lane_total = jnp.broadcast_to(row_total[..., None], row_total.shape + (HD,)).reshape(
        rows_here, requests, width_here
    )
    attended = (summed / lane_total).astype(jnp.bfloat16)
    col_index = lax.axis_index("col")
    col_count = lax.axis_size("col")
    col_width = model_width // col_count
    token_count = rows_here * requests
    attn_chunks = jnp.einsum(
        "tk,kcw->ctw",
        attended.reshape(token_count, width_here),
        out_weight.reshape(width_here, col_count, col_width),
        preferred_element_type=jnp.float32,
    ).astype(jnp.bfloat16)
    attn_summed = jnp.sum(
        lax.all_to_all(attn_chunks, "col", 0, 0, tiled=True).astype(jnp.float32), axis=0
    )
    residual_here = lax.dynamic_slice_in_dim(
        residual.reshape(token_count, model_width), col_index * col_width, col_width, 1
    )
    mixed_slice = (residual_here.astype(jnp.float32) + attn_summed).astype(jnp.bfloat16)
    mixed_gathered = lax.all_to_all(
        jnp.broadcast_to(mixed_slice[None], (col_count, token_count, col_width)),
        "col",
        0,
        0,
        tiled=True,
    )
    mixed_full = mixed_gathered.transpose(1, 0, 2).reshape(token_count, model_width)
    mixed_f32 = mixed_full.astype(jnp.float32)
    normed = (
        mixed_f32
        * lax.rsqrt(jnp.mean(mixed_f32 * mixed_f32, axis=-1, keepdims=True) + 1e-06)
        * norm_gain
    ).astype(jnp.bfloat16)
    tokens = normed
    entries_here = w_gate.shape[0]
    experts_dev = max(1, entries_here // GROUPS)
    groups_dev = entries_here // experts_dev
    experts_per_row = col_count * entries_here // GROUPS
    slots = row_count * experts_dev * CAP
    chosen = expert_ids.reshape(token_count * TOPK)
    onehot = (chosen[:, None] == jnp.arange(E, dtype=jnp.int32)[None, :]).astype(jnp.int32)
    slot_index = jnp.sum(jnp.cumsum(onehot, axis=0) * onehot, axis=1) - 1
    dest_row = chosen // experts_per_row
    local_expert = chosen - (dest_row * col_count + col_index) * entries_here // GROUPS
    valid = (local_expert >= 0) & (local_expert < experts_dev)
    place = (dest_row * experts_dev + local_expert) * CAP + slot_index
    place = jnp.where(valid, place, -1).reshape(token_count, TOPK)
    hit = place[:, :, None] == jnp.arange(slots, dtype=jnp.int32)[None, None, :]
    dispatch = jnp.sum(hit.astype(jnp.float32), axis=1).astype(jnp.bfloat16)
    combine = jnp.sum(
        jnp.where(hit, gate_values.reshape(token_count, TOPK, 1), 0.0), axis=1
    )
    outgoing = lax.dot_general(
        dispatch, tokens, (((0,), (0,)), ((), ())), preferred_element_type=jnp.float32
    ).astype(jnp.bfloat16)
    outgoing = outgoing.reshape(row_count, experts_dev, CAP, model_width)
    arrived = lax.all_to_all(outgoing, "row", 0, 0, tiled=True)
    shared_g = jnp.dot(tokens, shared_gate, preferred_element_type=jnp.float32)
    shared_u = jnp.dot(tokens, shared_up, preferred_element_type=jnp.float32)
    shared_act = (jax.nn.silu(shared_g) * shared_u).astype(jnp.bfloat16)
    shared_part = jnp.dot(shared_act, shared_down, preferred_element_type=jnp.float32)
    arrived, shared_part = lax.optimization_barrier((arrived, shared_part))
    hidden = w_gate.shape[2]
    wg = w_gate.reshape(experts_dev, groups_dev, model_width, hidden)
    wu = w_up.reshape(experts_dev, groups_dev, model_width, hidden)
    wd = w_down.reshape(experts_dev, groups_dev, hidden, model_width)
    combine_hi = (
        lax.reduce_precision(combine, exponent_bits=8, mantissa_bits=7)
        .astype(jnp.bfloat16)
        .reshape(token_count, row_count, experts_dev, CAP)
    )
    combine_lo = (
        (combine - lax.reduce_precision(combine, exponent_bits=8, mantissa_bits=7))
        .astype(jnp.bfloat16)
        .reshape(token_count, row_count, experts_dev, CAP)
    )
    routed = jnp.zeros((token_count, model_width), jnp.float32)
    for chunk in range(experts_dev):
        rows_in = arrived[:, chunk].reshape(row_count * CAP, model_width)
        gate_proj = jnp.einsum(
            "td,gdf->gtf", rows_in, wg[chunk], preferred_element_type=jnp.float32
        )
        up_proj = jnp.einsum("td,gdf->gtf", rows_in, wu[chunk], preferred_element_type=jnp.float32)
        hidden_act = lax.optimization_barrier(
            (jax.nn.silu(gate_proj) * up_proj).astype(jnp.bfloat16)
        )
        expert_out = jnp.einsum(
            "gtf,gfd->td", hidden_act, wd[chunk], preferred_element_type=jnp.float32
        ).astype(jnp.bfloat16)
        returned = lax.all_to_all(
            expert_out.reshape(row_count, CAP, model_width), "row", 0, 0, tiled=True
        ).reshape(row_count * CAP, model_width)
        pick_hi = combine_hi[:, :, chunk].reshape(token_count, row_count * CAP)
        pick_lo = combine_lo[:, :, chunk].reshape(token_count, row_count * CAP)
        routed = routed + (
            jnp.dot(pick_hi, returned, preferred_element_type=jnp.float32)
            + jnp.dot(pick_lo, returned, preferred_element_type=jnp.float32)
        )
    ffn_chunks = (
        (routed + shared_part)
        .astype(jnp.bfloat16)
        .reshape(token_count, col_count, col_width)
        .transpose(1, 0, 2)
    )
    ffn_total = jnp.sum(
        lax.all_to_all(ffn_chunks, "col", 0, 0, tiled=True).astype(jnp.float32), axis=0
    )
    ffn_here = ffn_total.astype(jnp.bfloat16).reshape(rows_here, requests, col_width)
    mixed_here = mixed_slice.reshape(rows_here, requests, col_width)
    return (mixed_here, ffn_here)


def solution(mesh):
    in_specs = (
        P("row", None, "col"),
        P("row", None, "col"),
        P("row", None, "col"),
        P("row", None, "col"),
        P("row", None, "col"),
        P(),
        P("row", None, None),
        P("col", None),
        P(),
        P("row", None, None),
        P("row", None, None),
        P(("row", "col"), None, None),
        P(("row", "col"), None, None),
        P(("row", "col"), None, None),
        P(None, "col"),
        P(None, "col"),
        P("col", None),
    )
    out_specs = (P("row", None, "col"), P("row", None, "col"))
    return jax.shard_map(body, mesh=mesh, in_specs=in_specs, out_specs=out_specs, check_vma=False)
```

```python
import math

import jax
import jax.numpy as jnp
from jax import lax
from jax.sharding import PartitionSpec as P

HD = 128
E = 64
TOPK = 6
GROUPS = 4
CAP = 24


def body(
    queries,
    new_keys,
    new_values,
    cache_keys,
    cache_values,
    cached_len,
    residual,
    out_weight,
    norm_gain,
    expert_ids,
    gate_values,
    w_gate,
    w_up,
    w_down,
    shared_gate,
    shared_up,
    shared_down,
):
    rows_here = queries.shape[0]
    requests = queries.shape[1]
    heads_here = queries.shape[2] // HD
    cache_rows = cache_keys.shape[0]
    block_rows = cache_rows + rows_here
    model_width = residual.shape[2]
    row_index = lax.axis_index("row")
    row_count = lax.axis_size("row")
    score_scale = 1.0 / math.sqrt(HD)
    key_pad = -(-block_rows // 128) * 128
    width_here = heads_here * HD
    keys_here = jnp.concatenate([cache_keys, new_keys], axis=0)
    values_here = jnp.concatenate([cache_values, new_values], axis=0)
    head_of_lane = jnp.arange(width_here, dtype=jnp.int32) // HD
    head_of_col = jnp.arange(heads_here * key_pad, dtype=jnp.int32) // key_pad
    block_mask = head_of_lane[:, None] == head_of_col[None, :]
    keys_t = jnp.pad(keys_here.transpose(1, 2, 0), ((0, 0), (0, 0), (0, key_pad - block_rows)))
    keys_block = jnp.where(
        block_mask[None], jnp.tile(keys_t, (1, 1, heads_here)), jnp.zeros((), keys_here.dtype)
    )
    values_t = jnp.pad(values_here.transpose(1, 0, 2), ((0, 0), (0, key_pad - block_rows), (0, 0)))
    values_block = jnp.where(
        block_mask.T[None], jnp.tile(values_t, (1, heads_here, 1)), jnp.zeros((), values_here.dtype)
    )
    all_queries = lax.all_to_all(
        jnp.broadcast_to(queries[None], (row_count,) + queries.shape), "row", 0, 0, tiled=True
    )
    query_count = row_count * rows_here
    query_rows = all_queries.reshape(query_count, requests, width_here)
    query_pos = jnp.arange(query_count, dtype=jnp.int32)
    offset_rows = jnp.arange(key_pad, dtype=jnp.int32)
    in_cache = offset_rows < cache_rows
    in_block = offset_rows < block_rows
    cache_pos = row_index * cache_rows + offset_rows
    new_pos = row_index * rows_here + offset_rows - cache_rows
    cache_ok = in_cache[None, :] & (cache_pos[None, :] < cached_len[:, None])
    new_ok = (
        jnp.logical_not(in_cache) & in_block
    )[None, :] & (new_pos[None, :] <= query_pos[:, None])
    allowed = cache_ok[:, None, None, :] | new_ok[None, :, None, :]
    scores = (
        jnp.einsum("irk,rkc->ric", query_rows, keys_block, preferred_element_type=jnp.float32)
        * score_scale
    ).reshape(requests, query_count, heads_here, key_pad)
    masked = jnp.where(allowed, scores, -1e30)
    block_max = jnp.max(masked, axis=-1)
    weights_now = jnp.where(allowed, jnp.exp(masked - block_max[..., None]), 0.0)
    block_sum = jnp.sum(weights_now, axis=-1)
    product = jnp.einsum(
        "ric,rck->irk",
        weights_now.astype(jnp.bfloat16).reshape(requests, query_count, heads_here * key_pad),
        values_block,
        preferred_element_type=jnp.float32,
    ).astype(jnp.bfloat16)
    stats = jnp.stack([block_max, block_sum], axis=-1).transpose(1, 0, 2, 3)
    product_back = lax.all_to_all(
        product.reshape(row_count, rows_here, requests, width_here), "row", 0, 0, tiled=True
    )
    stats_back = lax.all_to_all(
        stats.reshape(row_count, rows_here, requests, heads_here, 2), "row", 0, 0, tiled=True
    )
    part_max = stats_back[..., 0]
    row_top = jnp.max(part_max, axis=0)
    rescale = jnp.exp(part_max - row_top[None])
    row_total = jnp.sum(rescale * stats_back[..., 1], axis=0)
    lane_scale = jnp.broadcast_to(
        rescale[..., None], rescale.shape + (HD,)
    ).reshape(row_count, rows_here, requests, width_here)
    summed = jnp.sum(lane_scale * product_back.astype(jnp.float32), axis=0)
    lane_total = jnp.broadcast_to(row_total[..., None], row_total.shape + (HD,)).reshape(
        rows_here, requests, width_here
    )
    attended = (summed / lane_total).astype(jnp.bfloat16)
    col_index = lax.axis_index("col")
    col_count = lax.axis_size("col")
    col_width = model_width // col_count
    token_count = rows_here * requests
    attn_chunks = jnp.einsum(
        "tk,kcw->ctw",
        attended.reshape(token_count, width_here),
        out_weight.reshape(width_here, col_count, col_width),
        preferred_element_type=jnp.float32,
    ).astype(jnp.bfloat16)
    attn_summed = jnp.sum(
        lax.all_to_all(attn_chunks, "col", 0, 0, tiled=True).astype(jnp.float32), axis=0
    )
    residual_here = lax.dynamic_slice_in_dim(
        residual.reshape(token_count, model_width), col_index * col_width, col_width, 1
    )
    mixed_slice = (residual_here.astype(jnp.float32) + attn_summed).astype(jnp.bfloat16)
    mixed_gathered = lax.all_to_all(
        jnp.broadcast_to(mixed_slice[None], (col_count, token_count, col_width)),
        "col",
        0,
        0,
        tiled=True,
    )
    mixed_full = mixed_gathered.transpose(1, 0, 2).reshape(token_count, model_width)
    mixed_f32 = mixed_full.astype(jnp.float32)
    normed = (
        mixed_f32
        * lax.rsqrt(jnp.mean(mixed_f32 * mixed_f32, axis=-1, keepdims=True) + 1e-06)
        * norm_gain
    ).astype(jnp.bfloat16)
    tokens = normed
    entries_here = w_gate.shape[0]
    experts_dev = max(1, entries_here // GROUPS)
    groups_dev = entries_here // experts_dev
    experts_per_row = col_count * entries_here // GROUPS
    slots = row_count * experts_dev * CAP
    chosen = expert_ids.reshape(token_count * TOPK)
    onehot = (chosen[:, None] == jnp.arange(E, dtype=jnp.int32)[None, :]).astype(jnp.int32)
    slot_index = jnp.sum(jnp.cumsum(onehot, axis=0) * onehot, axis=1) - 1
    dest_row = chosen // experts_per_row
    local_expert = chosen - (dest_row * col_count + col_index) * entries_here // GROUPS
    valid = (local_expert >= 0) & (local_expert < experts_dev)
    place = (local_expert * row_count + dest_row) * CAP + slot_index
    place = jnp.where(valid, place, -1).reshape(token_count, TOPK)
    hit = place[:, :, None] == jnp.arange(slots, dtype=jnp.int32)[None, None, :]
    dispatch = jnp.sum(hit.astype(jnp.float32), axis=1).astype(jnp.bfloat16)
    combine = jnp.sum(
        jnp.where(hit, gate_values.reshape(token_count, TOPK, 1), 0.0), axis=1
    )
    outgoing = lax.dot_general(
        dispatch, tokens, (((0,), (0,)), ((), ())), preferred_element_type=jnp.float32
    ).astype(jnp.bfloat16)
    outgoing = outgoing.reshape(experts_dev, row_count, CAP, model_width)
    arrived = [
        lax.all_to_all(outgoing[chunk], "row", 0, 0, tiled=True) for chunk in range(experts_dev)
    ]
    shared_g = jnp.dot(tokens, shared_gate, preferred_element_type=jnp.float32)
    shared_u = jnp.dot(tokens, shared_up, preferred_element_type=jnp.float32)
    shared_act = (jax.nn.silu(shared_g) * shared_u).astype(jnp.bfloat16)
    shared_part = jnp.dot(shared_act, shared_down, preferred_element_type=jnp.float32)
    first_arrived, shared_part = lax.optimization_barrier((arrived[0], shared_part))
    arrived[0] = first_arrived
    hidden = w_gate.shape[2]
    wg = w_gate.reshape(experts_dev, groups_dev, model_width, hidden)
    wu = w_up.reshape(experts_dev, groups_dev, model_width, hidden)
    wd = w_down.reshape(experts_dev, groups_dev, hidden, model_width)
    combine_hi = combine.astype(jnp.bfloat16).reshape(token_count, experts_dev, row_count, CAP)
    combine_lo = (combine - combine_hi.reshape(token_count, slots).astype(jnp.float32)).astype(
        jnp.bfloat16
    ).reshape(token_count, experts_dev, row_count, CAP)
    routed = jnp.zeros((token_count, model_width), jnp.float32)
    for chunk in range(experts_dev):
        rows_in = arrived[chunk].reshape(row_count * CAP, model_width)
        gate_proj = jnp.einsum(
            "td,gdf->gtf", rows_in, wg[chunk], preferred_element_type=jnp.float32
        )
        up_proj = jnp.einsum("td,gdf->gtf", rows_in, wu[chunk], preferred_element_type=jnp.float32)
        hidden_act = lax.optimization_barrier(
            (jax.nn.silu(gate_proj) * up_proj).astype(jnp.bfloat16)
        )
        expert_out = jnp.einsum(
            "gtf,gfd->td", hidden_act, wd[chunk], preferred_element_type=jnp.float32
        ).astype(jnp.bfloat16)
        returned = lax.all_to_all(
            expert_out.reshape(row_count, CAP, model_width), "row", 0, 0, tiled=True
        ).reshape(row_count * CAP, model_width)
        pick_hi = combine_hi[:, chunk].reshape(token_count, row_count * CAP)
        pick_lo = combine_lo[:, chunk].reshape(token_count, row_count * CAP)
        routed = routed + (
            jnp.dot(pick_hi, returned, preferred_element_type=jnp.float32)
            + jnp.dot(pick_lo, returned, preferred_element_type=jnp.float32)
        )
    ffn_chunks = (
        (routed + shared_part)
        .astype(jnp.bfloat16)
        .reshape(token_count, col_count, col_width)
        .transpose(1, 0, 2)
    )
    ffn_total = jnp.sum(
        lax.all_to_all(ffn_chunks, "col", 0, 0, tiled=True).astype(jnp.float32), axis=0
    )
    ffn_here = ffn_total.astype(jnp.bfloat16).reshape(rows_here, requests, col_width)
    mixed_here = mixed_slice.reshape(rows_here, requests, col_width)
    return (mixed_here, ffn_here)


def solution(mesh):
    in_specs = (
        P("row", None, "col"),
        P("row", None, "col"),
        P("row", None, "col"),
        P("row", None, "col"),
        P("row", None, "col"),
        P(),
        P("row", None, None),
        P("col", None),
        P(),
        P("row", None, None),
        P("row", None, None),
        P(("row", "col"), None, None),
        P(("row", "col"), None, None),
        P(("row", "col"), None, None),
        P(None, "col"),
        P(None, "col"),
        P("col", None),
    )
    out_specs = (P("row", None, "col"), P("row", None, "col"))
    return jax.shard_map(body, mesh=mesh, in_specs=in_specs, out_specs=out_specs, check_vma=False)
```

```python
import math

import jax
import jax.numpy as jnp
from jax import lax
from jax.sharding import PartitionSpec as P

HD = 128
E = 64
TOPK = 6
GROUPS = 4
CAP = 24


def body(
    queries,
    new_keys,
    new_values,
    cache_keys,
    cache_values,
    cached_len,
    residual,
    out_weight,
    norm_gain,
    expert_ids,
    gate_values,
    w_gate,
    w_up,
    w_down,
    shared_gate,
    shared_up,
    shared_down,
):
    rows_here = queries.shape[0]
    requests = queries.shape[1]
    heads_here = queries.shape[2] // HD
    cache_rows = cache_keys.shape[0]
    block_rows = cache_rows + rows_here
    model_width = residual.shape[2]
    row_index = lax.axis_index("row")
    row_count = lax.axis_size("row")
    score_scale = 1.0 / math.sqrt(HD)
    key_pad = -(-block_rows // 128) * 128
    width_here = heads_here * HD
    keys_here = jnp.concatenate([cache_keys, new_keys], axis=0)
    values_here = jnp.concatenate([cache_values, new_values], axis=0)
    head_of_lane = jnp.arange(width_here, dtype=jnp.int32) // HD
    head_of_col = jnp.arange(heads_here * key_pad, dtype=jnp.int32) // key_pad
    block_mask = head_of_lane[:, None] == head_of_col[None, :]
    keys_t = jnp.pad(keys_here.transpose(1, 2, 0), ((0, 0), (0, 0), (0, key_pad - block_rows)))
    keys_block = jnp.where(
        block_mask[None], jnp.tile(keys_t, (1, 1, heads_here)), jnp.zeros((), keys_here.dtype)
    )
    values_t = jnp.pad(values_here.transpose(1, 0, 2), ((0, 0), (0, key_pad - block_rows), (0, 0)))
    values_block = jnp.where(
        block_mask.T[None], jnp.tile(values_t, (1, heads_here, 1)), jnp.zeros((), values_here.dtype)
    )
    all_queries = lax.all_to_all(
        jnp.broadcast_to(queries[None], (row_count,) + queries.shape), "row", 0, 0, tiled=True
    )
    query_count = row_count * rows_here
    query_rows = all_queries.reshape(query_count, requests, width_here)
    query_pos = jnp.arange(query_count, dtype=jnp.int32)
    offset_rows = jnp.arange(key_pad, dtype=jnp.int32)
    in_cache = offset_rows < cache_rows
    in_block = offset_rows < block_rows
    cache_pos = row_index * cache_rows + offset_rows
    new_pos = row_index * rows_here + offset_rows - cache_rows
    cache_ok = in_cache[None, :] & (cache_pos[None, :] < cached_len[:, None])
    new_ok = (
        jnp.logical_not(in_cache) & in_block
    )[None, :] & (new_pos[None, :] <= query_pos[:, None])
    allowed = cache_ok[:, None, None, :] | new_ok[None, :, None, :]
    scores = (
        jnp.einsum("irk,rkc->ric", query_rows, keys_block, preferred_element_type=jnp.float32)
        * score_scale
    ).reshape(requests, query_count, heads_here, key_pad)
    masked = jnp.where(allowed, scores, -1e30)
    block_max = jnp.max(masked, axis=-1)
    weights_now = jnp.where(allowed, jnp.exp(masked - block_max[..., None]), 0.0)
    block_sum = jnp.sum(weights_now, axis=-1)
    product = jnp.einsum(
        "ric,rck->irk",
        weights_now.astype(jnp.bfloat16).reshape(requests, query_count, heads_here * key_pad),
        values_block,
        preferred_element_type=jnp.float32,
    ).astype(jnp.bfloat16)
    stats = jnp.stack([block_max, block_sum], axis=-1).transpose(1, 0, 2, 3)
    product_back = lax.all_to_all(
        product.reshape(row_count, rows_here, requests, width_here), "row", 0, 0, tiled=True
    )
    stats_back = lax.all_to_all(
        stats.reshape(row_count, rows_here, requests, heads_here, 2), "row", 0, 0, tiled=True
    )
    part_max = stats_back[..., 0]
    row_top = jnp.max(part_max, axis=0)
    rescale = jnp.exp(part_max - row_top[None])
    row_total = jnp.sum(rescale * stats_back[..., 1], axis=0)
    lane_scale = jnp.broadcast_to(
        rescale[..., None], rescale.shape + (HD,)
    ).reshape(row_count, rows_here, requests, width_here)
    summed = jnp.sum(lane_scale * product_back.astype(jnp.float32), axis=0)
    lane_total = jnp.broadcast_to(row_total[..., None], row_total.shape + (HD,)).reshape(
        rows_here, requests, width_here
    )
    attended = (summed / lane_total).astype(jnp.bfloat16)
    col_index = lax.axis_index("col")
    col_count = lax.axis_size("col")
    col_width = model_width // col_count
    token_count = rows_here * requests
    attn_chunks = jnp.einsum(
        "tk,kcw->ctw",
        attended.reshape(token_count, width_here),
        out_weight.reshape(width_here, col_count, col_width),
        preferred_element_type=jnp.float32,
    ).astype(jnp.bfloat16)
    attn_summed = jnp.sum(
        lax.all_to_all(attn_chunks, "col", 0, 0, tiled=True).astype(jnp.float32), axis=0
    )
    residual_here = lax.dynamic_slice_in_dim(
        residual.reshape(token_count, model_width), col_index * col_width, col_width, 1
    )
    mixed_slice = (residual_here.astype(jnp.float32) + attn_summed).astype(jnp.bfloat16)
    mixed_gathered = lax.all_to_all(
        jnp.broadcast_to(mixed_slice[None], (col_count, token_count, col_width)),
        "col",
        0,
        0,
        tiled=True,
    )
    mixed_full = mixed_gathered.transpose(1, 0, 2).reshape(token_count, model_width)
    mixed_f32 = mixed_full.astype(jnp.float32)
    normed = (
        mixed_f32
        * lax.rsqrt(jnp.mean(mixed_f32 * mixed_f32, axis=-1, keepdims=True) + 1e-06)
        * norm_gain
    ).astype(jnp.bfloat16)
    tokens = normed
    entries_here = w_gate.shape[0]
    experts_dev = max(1, entries_here // GROUPS)
    groups_dev = entries_here // experts_dev
    experts_per_row = col_count * entries_here // GROUPS
    slots = row_count * experts_dev * CAP
    chosen = expert_ids.reshape(token_count * TOPK)
    onehot = (chosen[:, None] == jnp.arange(E, dtype=jnp.int32)[None, :]).astype(jnp.int32)
    slot_index = jnp.sum(jnp.cumsum(onehot, axis=0) * onehot, axis=1) - 1
    dest_row = chosen // experts_per_row
    local_expert = chosen - (dest_row * col_count + col_index) * entries_here // GROUPS
    valid = (local_expert >= 0) & (local_expert < experts_dev)
    place = (local_expert * row_count + dest_row) * CAP + slot_index
    place = jnp.where(valid, place, -1).reshape(token_count, TOPK)
    hit = place[:, :, None] == jnp.arange(slots, dtype=jnp.int32)[None, None, :]
    dispatch = jnp.sum(hit.astype(jnp.float32), axis=1).astype(jnp.bfloat16)
    combine = jnp.sum(
        jnp.where(hit, gate_values.reshape(token_count, TOPK, 1), 0.0), axis=1
    )
    chunk_width = row_count * CAP
    arrived = [
        lax.all_to_all(
            lax.dot_general(
                dispatch[:, chunk * chunk_width : (chunk + 1) * chunk_width],
                tokens,
                (((0,), (0,)), ((), ())),
                preferred_element_type=jnp.float32,
            )
            .astype(jnp.bfloat16)
            .reshape(row_count, CAP, model_width),
            "row",
            0,
            0,
            tiled=True,
        )
        for chunk in range(experts_dev)
    ]
    shared_g = jnp.dot(tokens, shared_gate, preferred_element_type=jnp.float32)
    shared_u = jnp.dot(tokens, shared_up, preferred_element_type=jnp.float32)
    shared_act = (jax.nn.silu(shared_g) * shared_u).astype(jnp.bfloat16)
    shared_part = jnp.dot(shared_act, shared_down, preferred_element_type=jnp.float32)
    first_arrived, shared_part = lax.optimization_barrier((arrived[0], shared_part))
    arrived[0] = first_arrived
    hidden = w_gate.shape[2]
    wg = w_gate.reshape(experts_dev, groups_dev, model_width, hidden)
    wu = w_up.reshape(experts_dev, groups_dev, model_width, hidden)
    wd = w_down.reshape(experts_dev, groups_dev, hidden, model_width)
    combine_hi = combine.astype(jnp.bfloat16).reshape(token_count, experts_dev, row_count, CAP)
    combine_lo = (combine - combine_hi.reshape(token_count, slots).astype(jnp.float32)).astype(
        jnp.bfloat16
    ).reshape(token_count, experts_dev, row_count, CAP)
    routed = jnp.zeros((token_count, model_width), jnp.float32)
    for chunk in range(experts_dev):
        rows_in = arrived[chunk].reshape(row_count * CAP, model_width)
        gate_proj = jnp.einsum(
            "td,gdf->gtf", rows_in, wg[chunk], preferred_element_type=jnp.float32
        )
        up_proj = jnp.einsum("td,gdf->gtf", rows_in, wu[chunk], preferred_element_type=jnp.float32)
        hidden_act = lax.optimization_barrier(
            (jax.nn.silu(gate_proj) * up_proj).astype(jnp.bfloat16)
        )
        expert_out = jnp.einsum(
            "gtf,gfd->td", hidden_act, wd[chunk], preferred_element_type=jnp.float32
        ).astype(jnp.bfloat16)
        returned = lax.all_to_all(
            expert_out.reshape(row_count, CAP, model_width), "row", 0, 0, tiled=True
        ).reshape(row_count * CAP, model_width)
        pick_hi = combine_hi[:, chunk].reshape(token_count, row_count * CAP)
        pick_lo = combine_lo[:, chunk].reshape(token_count, row_count * CAP)
        routed = routed + (
            jnp.dot(pick_hi, returned, preferred_element_type=jnp.float32)
            + jnp.dot(pick_lo, returned, preferred_element_type=jnp.float32)
        )
    ffn_chunks = (
        (routed + shared_part)
        .astype(jnp.bfloat16)
        .reshape(token_count, col_count, col_width)
        .transpose(1, 0, 2)
    )
    ffn_total = jnp.sum(
        lax.all_to_all(ffn_chunks, "col", 0, 0, tiled=True).astype(jnp.float32), axis=0
    )
    ffn_here = ffn_total.astype(jnp.bfloat16).reshape(rows_here, requests, col_width)
    mixed_here = mixed_slice.reshape(rows_here, requests, col_width)
    return (mixed_here, ffn_here)


def solution(mesh):
    in_specs = (
        P("row", None, "col"),
        P("row", None, "col"),
        P("row", None, "col"),
        P("row", None, "col"),
        P("row", None, "col"),
        P(),
        P("row", None, None),
        P("col", None),
        P(),
        P("row", None, None),
        P("row", None, None),
        P(("row", "col"), None, None),
        P(("row", "col"), None, None),
        P(("row", "col"), None, None),
        P(None, "col"),
        P(None, "col"),
        P("col", None),
    )
    out_specs = (P("row", None, "col"), P("row", None, "col"))
    return jax.shard_map(body, mesh=mesh, in_specs=in_specs, out_specs=out_specs, check_vma=False)
```
